256 devices in a mesh: rows: 64 (over z, y, core), shock: 4 (over x).
Axes of the slice: x: 4, y: 4, z: 8, core: 2. Of those that a mesh axis runs over, the one named last changes fastest.
Arguments:
- coefs: bfloat16 [256, 16, 128, 128], P('rows'), may hold values from -0.125 to 0.125
- lag_pattern: int32 [256, 16], replicated, may hold values from 0 to 255, as said below
- loadings: float32 [32768, 128], P('rows'), may hold values from -0.5 to 0.5
- idiosyncratic: float32 [32768], P('rows'), may hold values from 0.5 to 2
- shocked: int32 [512], P('shock'), may hold values from 0 to 32767
Outputs:
- shares: float32 [32768, 512], P('rows', 'shock')
The draws below stay inside these ranges and needn't reach their ends.
Inputs may be any that keep to these rules, and one draw needn't show every extreme that they name: `lag_pattern`: each row holds distinct blocks. The block rows held by any one device along `rows` together read exactly 1 distinct block from the 4 blocks held by every device along `rows`.
All inputs are finite; a program needn't handle non-finite values.
Results may differ from the reference program's by a relative error of at most 0.009.
Values may be sent and summed in bfloat16 or wider, within the bound.
No kernel may reach another device: no remote copies, remote signals or barrier semaphores. Data moves between devices by JAX's collectives and lax.ppermute only.
A program may use at most 64 MiB of HBM per device.

```python
import math
import jax
import jax.numpy as jnp
from jax import lax

BSZ = 128
LAGS = 16
FACTORS = 128
BLK_DEV = 4
HORIZONS = 7
BLOCKS = 256
ASSET_COUNT = 32768
SHOCK_COUNT = 512
CAP = 1


def draw_lag_pattern(key, part):
    owners = BLOCKS // BLK_DEV
    total = owners * CAP
    first_key, second_key = jax.random.split(key)
    scores = jax.random.randint(first_key, (owners, owners, BLK_DEV), 0, 1 << 20) * BLK_DEV + jnp.arange(BLK_DEV, dtype=jnp.int32)
    order = jnp.argsort(scores, axis=-1, stable=True)[:, :, :CAP]
    block_ids = (jnp.arange(owners, dtype=jnp.int32)[None, :, None] * BLK_DEV + order).reshape(owners, total)
    mixing = jax.random.randint(second_key, (owners, total), 0, 1 << 20) * total + jnp.arange(total, dtype=jnp.int32)
    shuffle = jnp.argsort(mixing, axis=-1, stable=True)
    block_ids = jnp.take_along_axis(block_ids, shuffle, axis=1)
    slot_pos = jnp.arange(BLK_DEV * LAGS, dtype=jnp.int32) % total
    return block_ids[:, slot_pos].reshape(BLOCKS, LAGS).astype(jnp.int32)


def set_ends(entries, key, low, top_value):
    longest = entries.shape.index(max(entries.shape))
    spots = []
    for shift in (0, 1):
        where = [jax.random.randint(jax.random.fold_in(key, axis), (), 0, length) for axis, length in enumerate(entries.shape)]
        where[longest] = (where[longest] + shift) % entries.shape[longest]
        spots.append(tuple(where))
    return entries.at[spots[0]].set(low).at[spots[1]].set(top_value)


def block_scale(own_key, extent, cuts, least, high):
    def one(dim, shards_of):
        heights = jax.random.uniform(jax.random.fold_in(jax.random.fold_in(own_key, 6), dim), (shards_of,), jnp.float32, least / len(cuts), high / len(cuts))
        return jnp.repeat(jnp.exp(heights), extent[dim] // shards_of).reshape((-1,) + (1,) * (len(extent) - dim - 1))

    gain = one(*cuts[0])
    for cut in cuts[1:]:
        gain = gain * one(*cut)
    return gain


def gaussian(key, shape, width, limit, shards=(), held_as=jnp.bfloat16):
    values = width * jax.random.normal(key, shape, jnp.float32)
    if shards:
        values = values * block_scale(key, shape, shards, -0.22, 0.18)
    return jnp.clip(values, -limit, limit).astype(held_as)


def setup_inputs(seed: int = 0) -> dict:
    splits = jax.random.split(jax.random.key(seed), 6)
    coefs = gaussian(splits[0], (BLOCKS, LAGS, BSZ, BSZ), (LAGS * BSZ) ** -0.5, 0.125, ((0, 64),))
    lag_pattern = draw_lag_pattern(jax.random.fold_in(splits[5], 71), 0)
    loadings = gaussian(splits[2], (ASSET_COUNT, FACTORS), FACTORS ** -0.5, 0.5, ((0, 64),), jnp.float32)
    idiosyncratic = jnp.clip(jnp.exp(math.log(2.0) - 1.3862944 * jax.random.uniform(splits[3], (ASSET_COUNT,), jnp.float32) ** block_scale(splits[3], (ASSET_COUNT,), ((0, 64),), -0.2, 0.2)), 0.5, 2.0)
    shocked = set_ends(jax.random.randint(splits[4], (SHOCK_COUNT,), 0, ASSET_COUNT), jax.random.fold_in(splits[4], 1), 0, ASSET_COUNT - 1).astype(jnp.int32)
    return dict(coefs=coefs, lag_pattern=lag_pattern, loadings=loadings, idiosyncratic=idiosyncratic, shocked=shocked)


def reference(coefs, lag_pattern, loadings, idiosyncratic, shocked):
    picked = loadings[shocked]
    picked_idio = idiosyncratic[shocked]
    scale = jnp.sqrt(lax.optimization_barrier(jnp.sum(picked * picked, axis=1)) + picked_idio)
    assets = loadings.shape[0]
    positions = jnp.arange(assets, dtype=jnp.int32)
    diagonal_hit = (positions[:, None] == shocked[None, :]).astype(jnp.float32)
    impact = jnp.dot(loadings, picked.T, precision=lax.Precision.HIGHEST, preferred_element_type=jnp.float32)
    impact = impact + diagonal_hit * idiosyncratic[:, None]
    impact = impact / scale[None, :]
    present_response = impact.astype(jnp.bfloat16).reshape(BLOCKS, BSZ, SHOCK_COUNT)
    squared_terms = present_response.astype(jnp.float32) ** 2
    for step in range(HORIZONS - 1):

        def one_row(packed, source=present_response):
            row_coef, row_lags = packed
            lagged = source[row_lags].astype(jnp.float32)
            product = jnp.einsum('lij,ljs->is', row_coef.astype(jnp.float32), lagged)
            return product.astype(jnp.bfloat16)
        present_response = lax.map(one_row, (coefs, lag_pattern))
        squared_terms = squared_terms + present_response.astype(jnp.float32) ** 2
    totals = lax.optimization_barrier(jnp.sum(squared_terms, axis=2))
    shares = SHOCK_COUNT * squared_terms / (totals[:, :, None] + 1e-06)
    return shares.reshape(ASSET_COUNT, SHOCK_COUNT)
```

```python
import jax
import jax.numpy as jnp
from jax import lax
from jax.sharding import PartitionSpec as P

HORIZONS = 7


def gather_rows(chosen, chosen_idio, owners):
    shocks, factors = chosen.shape
    per = shocks // owners
    packed = jnp.concatenate(
        [
            chosen.reshape(owners, per, factors),
            jnp.pad(chosen_idio.reshape(owners, 1, per), ((0, 0), (0, 0), (0, factors - per))),
        ],
        axis=1,
    )
    arrived = lax.all_to_all(packed, "rows", 0, 0, tiled=True)
    reduced = jnp.sum(arrived, axis=0, keepdims=True)
    spread = jnp.broadcast_to(reduced, packed.shape)
    full = lax.all_to_all(spread, "rows", 0, 0, tiled=True)
    return full[:, :per, :].reshape(shocks, factors), full[:, per, :per].reshape(shocks)


def on_device(coefs, lag_pattern, loadings, idiosyncratic, shocked):
    blk_dev = coefs.shape[0]
    lags = coefs.shape[1]
    block_size = coefs.shape[2]
    owners = lax.axis_size("rows")
    mine = lax.axis_index("rows")
    n_blocks = owners * blk_dev
    capacity = min(blk_dev, max(1, blk_dev * lags // owners))
    shock_columns = shocked.shape[0]
    local_rows = blk_dev * block_size
    row_ids = mine * local_rows + jnp.arange(local_rows, dtype=jnp.int32)
    pick_table = (shocked[:, None] == row_ids[None, :]).astype(jnp.float32)
    chosen = jnp.dot(
        pick_table, loadings, precision=lax.Precision.HIGHEST, preferred_element_type=jnp.float32
    )
    chosen_idio = jnp.dot(
        pick_table,
        idiosyncratic,
        precision=lax.Precision.HIGHEST,
        preferred_element_type=jnp.float32,
    )
    chosen, chosen_idio = gather_rows(chosen, chosen_idio, owners)
    scale = jnp.sqrt(jnp.sum(chosen * chosen, axis=1) + chosen_idio)
    impact = jnp.dot(
        loadings, chosen.T, precision=lax.Precision.HIGHEST, preferred_element_type=jnp.float32
    )
    impact = impact + pick_table.T * idiosyncratic[:, None]
    impact = impact / scale[None, :]
    present_response = impact.astype(jnp.bfloat16).reshape(blk_dev, block_size, shock_columns)
    squared_terms = present_response.astype(jnp.float32) ** 2
    my_lags = lax.dynamic_slice_in_dim(lag_pattern, mine * blk_dev, blk_dev, 0)
    flat_lags = my_lags.reshape(-1)
    all_blocks_ids = jnp.arange(n_blocks, dtype=jnp.int32)
    read_need = jnp.any(flat_lags[:, None] == all_blocks_ids[None, :], axis=0).astype(jnp.int32)
    read_need = read_need.reshape(owners, blk_dev)
    read_before = jnp.cumsum(read_need, axis=1) - read_need
    owner_base = jnp.arange(owners, dtype=jnp.int32)[:, None] * capacity
    slot_of_block = (owner_base + read_before).reshape(-1)
    take_index = slot_of_block[flat_lags]
    reader_slots = lag_pattern.reshape(owners, blk_dev * lags)
    own_ids = mine * blk_dev + jnp.arange(blk_dev, dtype=jnp.int32)
    send_need = jnp.any(reader_slots[:, :, None] == own_ids[None, None, :], axis=1).astype(
        jnp.int32
    )
    send_before = jnp.cumsum(send_need, axis=1) - send_need
    cap_pos = jnp.arange(capacity, dtype=jnp.int32)
    routing_matrix = (
        (send_need[:, None, :] == 1) & (send_before[:, None, :] == cap_pos[None, :, None])
    ).astype(jnp.bfloat16)
    for step in range(HORIZONS - 1):
        outgoing = jnp.einsum(
            "vwq,qfn->vwfn", routing_matrix, present_response, preferred_element_type=jnp.float32
        ).astype(jnp.bfloat16)
        arriving_response = lax.all_to_all(
            outgoing, "rows", split_axis=0, concat_axis=0, tiled=True
        )
        stacked = arriving_response.reshape(owners * capacity, block_size, shock_columns)
        lagged = jnp.take(stacked, take_index, axis=0).reshape(
            blk_dev, lags, block_size, shock_columns
        )
        product = jnp.einsum("rlij,rljs->ris", coefs, lagged, preferred_element_type=jnp.float32)
        present_response = product.astype(jnp.bfloat16)
        squared_terms = squared_terms + present_response.astype(jnp.float32) ** 2
    totals = lax.psum(jnp.sum(squared_terms, axis=2), "shock")
    total_shocks = shock_columns * lax.axis_size("shock")
    shares = total_shocks * squared_terms / (totals[:, :, None] + 1e-06)
    return shares.reshape(local_rows, shock_columns)


def solution(mesh):
    placed = (P("rows", None, None, None), P(), P("rows", None), P("rows"), P("shock"))
    return jax.shard_map(
        on_device, mesh=mesh, in_specs=placed, out_specs=P("rows", "shock"), check_vma=False
    )
```

```python
import numpy as np
import jax
import jax.numpy as jnp
from jax import lax
from jax.sharding import Mesh
from jax.sharding import PartitionSpec as P

HORIZONS = 7
CORE = 2
YS = 4
ZL = 2
ALL = ("zh", "zl", "y", "c", "x")
BOX = ("zl", "y", "c", "x")


def layout(zh, xs):
    zs = zh * ZL
    flat = lambda k, zl, y, c, x: (((k * ZL + zl) * YS + y) * CORE + c) * xs + x
    group_of = np.zeros((zh, ZL * YS * CORE * xs), np.int32)
    pos_of = np.zeros((zh, zs * YS * CORE), np.int32)
    zsrc = np.zeros((zh, ZL, YS, CORE, xs), np.int32)
    perm_in, perm_out = [], []
    for k in range(zh):
        for zl in range(ZL):
            for y in range(YS):
                for c in range(CORE):
                    for x in range(xs):
                        d = x if c == 0 else xs - 1 - x
                        z = (ZL * k - d) % zs if zl == 0 else (ZL * k + 1 + d) % zs
                        zsrc[k, zl, y, c, x] = z
                        g = (z * YS + y) * CORE + c
                        pos = ((zl * YS + y) * CORE + c) * xs + x
                        group_of[k, pos] = g
                        pos_of[k, g] = pos
                        src = flat(z // ZL, z % ZL, y, c, x)
                        me = flat(k, zl, y, c, x)
                        perm_in.append((src, me))
                        perm_out.append((me, flat(z // ZL, z % ZL, y, c, k)))
    return zsrc, group_of, pos_of, perm_in, perm_out


def gather_rows(chosen, chosen_idio, owners):
    shocks, factors = chosen.shape
    per = shocks // owners
    packed = jnp.concatenate(
        [
            chosen.reshape(owners, per, factors),
            jnp.pad(chosen_idio.reshape(owners, 1, per), ((0, 0), (0, 0), (0, factors - per))),
        ],
        axis=1,
    )
    arrived = lax.all_to_all(packed, BOX, 0, 0, tiled=True)
    reduced = jnp.sum(arrived, axis=0, keepdims=True)
    spread = jnp.broadcast_to(reduced, packed.shape)
    full = lax.all_to_all(spread, BOX, 0, 0, tiled=True)
    return full[:, :per, :].reshape(shocks, factors), full[:, per, :per].reshape(shocks)


def make_body(zh, xs):
    zsrc_t, group_t, pos_t, perm_in, perm_out = layout(zh, xs)

    def on_device(coefs, lag_pattern, loadings, idiosyncratic, shocked):
        loadings, idiosyncratic = lax.ppermute((loadings, idiosyncratic), ALL, perm_in)
        coefs = lax.ppermute(coefs, ALL, perm_in)
        blk_dev = coefs.shape[0]
        lags = coefs.shape[1]
        block_size = coefs.shape[2]
        k = lax.axis_index("zh")
        zl = lax.axis_index("zl")
        y = lax.axis_index("y")
        c = lax.axis_index("c")
        x = lax.axis_index("x")
        owners = ZL * YS * CORE * xs
        mine = (jnp.asarray(zsrc_t)[k, zl, y, c, x] * YS + y) * CORE + c
        group_of_pos = jnp.asarray(group_t)[k]
        pos_of_group = jnp.asarray(pos_t)[k]
        n_blocks = owners * blk_dev
        capacity = min(blk_dev, max(1, blk_dev * lags // owners))
        all_shocks = lax.all_gather(shocked, "x", axis=0, tiled=True)
        shock_columns = shocked.shape[0]
        shocked = lax.dynamic_slice_in_dim(all_shocks, k * shock_columns, shock_columns, 0)
        local_rows = blk_dev * block_size
        row_ids = mine * local_rows + jnp.arange(local_rows, dtype=jnp.int32)
        pick_table = (shocked[:, None] == row_ids[None, :]).astype(jnp.float32)
        chosen = jnp.dot(
            pick_table, loadings, precision=lax.Precision.HIGHEST, preferred_element_type=jnp.float32
        )
        chosen_idio = jnp.dot(
            pick_table,
            idiosyncratic,
            precision=lax.Precision.HIGHEST,
            preferred_element_type=jnp.float32,
        )
        chosen, chosen_idio = gather_rows(chosen, chosen_idio, owners)
        scale = jnp.sqrt(jnp.sum(chosen * chosen, axis=1) + chosen_idio)
        impact = jnp.dot(
            loadings, chosen.T, precision=lax.Precision.HIGHEST, preferred_element_type=jnp.float32
        )
        impact = impact + pick_table.T * idiosyncratic[:, None]
        impact = impact / scale[None, :]
        present_response = impact.astype(jnp.bfloat16).reshape(blk_dev, block_size, shock_columns)
        squared_terms = present_response.astype(jnp.float32) ** 2
        my_lags = lax.dynamic_slice_in_dim(lag_pattern, mine * blk_dev, blk_dev, 0)
        flat_lags = my_lags.reshape(-1)
        all_blocks_ids = jnp.arange(n_blocks, dtype=jnp.int32)
        read_need = jnp.any(flat_lags[:, None] == all_blocks_ids[None, :], axis=0).astype(jnp.int32)
        read_need = read_need.reshape(owners, blk_dev)[group_of_pos]
        read_before = jnp.cumsum(read_need, axis=1) - read_need
        owner_base = jnp.arange(owners, dtype=jnp.int32)[:, None] * capacity
        slot_of_pos = (owner_base + read_before).reshape(-1)
        block_at = pos_of_group[flat_lags // blk_dev] * blk_dev + flat_lags % blk_dev
        take_index = slot_of_pos[block_at]
        reader_slots = lag_pattern.reshape(owners, blk_dev * lags)[group_of_pos]
        own_ids = mine * blk_dev + jnp.arange(blk_dev, dtype=jnp.int32)
        send_need = jnp.any(reader_slots[:, :, None] == own_ids[None, None, :], axis=1).astype(
            jnp.int32
        )
        send_before = jnp.cumsum(send_need, axis=1) - send_need
        cap_pos = jnp.arange(capacity, dtype=jnp.int32)
        routing_matrix = (
            (send_need[:, None, :] == 1) & (send_before[:, None, :] == cap_pos[None, :, None])
        ).astype(jnp.bfloat16)
        for step in range(HORIZONS - 1):
            outgoing = jnp.einsum(
                "vwq,qfn->vwfn", routing_matrix, present_response, preferred_element_type=jnp.float32
            ).astype(jnp.bfloat16)
            arriving_response = lax.all_to_all(outgoing, BOX, split_axis=0, concat_axis=0, tiled=True)
            stacked = arriving_response.reshape(owners * capacity, block_size, shock_columns)
            lagged = jnp.take(stacked, take_index, axis=0).reshape(
                blk_dev, lags, block_size, shock_columns
            )
            product = jnp.einsum("rlij,rljs->ris", coefs, lagged, preferred_element_type=jnp.float32)
            present_response = product.astype(jnp.bfloat16)
            squared_terms = squared_terms + present_response.astype(jnp.float32) ** 2
        partial = jnp.sum(squared_terms, axis=2)
        squared_terms, partial = lax.ppermute((squared_terms, partial), ALL, perm_out)
        totals = lax.psum(partial, "x")
        total_shocks = shock_columns * xs
        shares = total_shocks * squared_terms / (totals[:, :, None] + 1e-06)
        return shares.reshape(local_rows, shock_columns)

    return on_device


def solution(mesh):
    rows = mesh.shape["rows"]
    xs = mesh.shape["shock"]
    zh = rows // (ZL * YS * CORE)
    mesh5 = Mesh(mesh.devices.reshape(zh, ZL, YS, CORE, xs), ALL)
    rows_axes = ("zh", "zl", "y", "c")
    placed = (
        P(rows_axes, None, None, None),
        P(),
        P(rows_axes, None),
        P(rows_axes),
        P("x"),
    )
    return jax.shard_map(
        make_body(zh, xs), mesh=mesh5, in_specs=placed, out_specs=P(rows_axes, "x"), check_vma=False
    )
```

```python
import numpy as np
import jax
import jax.numpy as jnp
from jax import lax
from jax.sharding import Mesh
from jax.sharding import PartitionSpec as P

HORIZONS = 7
CORE = 2
YS = 4
ZL = 2
ALL = ("zh", "zl", "y", "c", "x")
BOX = ("zl", "y", "c", "x")


def layout(zh, xs):
    zs = zh * ZL
    flat = lambda k, zl, y, c, x: (((k * ZL + zl) * YS + y) * CORE + c) * xs + x
    group_of = np.zeros((zh, ZL * YS * CORE * xs), np.int32)
    pos_of = np.zeros((zh, zs * YS * CORE), np.int32)
    zsrc = np.zeros((zh, ZL, YS, CORE, xs), np.int32)
    perm_in, perm_out = [], []
    for k in range(zh):
        for zl in range(ZL):
            for y in range(YS):
                for c in range(CORE):
                    for x in range(xs):
                        d = x if c == 0 else xs - 1 - x
                        z = (ZL * k - d) % zs if zl == 0 else (ZL * k + 1 + d) % zs
                        zsrc[k, zl, y, c, x] = z
                        g = (z * YS + y) * CORE + c
                        pos = ((zl * YS + y) * CORE + c) * xs + x
                        group_of[k, pos] = g
                        pos_of[k, g] = pos
                        src = flat(z // ZL, z % ZL, y, c, x)
                        me = flat(k, zl, y, c, x)
                        perm_in.append((src, me))
                        perm_out.append([(me, flat(z // ZL, z % ZL, y, c, (k + j) % xs)) for j in range(xs)])
    perm_out = [[p[j] for p in perm_out] for j in range(xs)]
    perm_x = [
        [(flat(k, zl, y, c, x), flat(k, zl, y, c, (x + j) % xs)) for k in range(zh) for zl in range(ZL)
         for y in range(YS) for c in range(CORE) for x in range(xs)]
        for j in range(xs)
    ]
    return zsrc, group_of, pos_of, perm_in, perm_out, perm_x


def gather_rows(chosen, chosen_idio, owners):
    shocks, factors = chosen.shape
    per = shocks // owners
    packed = jnp.concatenate(
        [
            chosen.reshape(owners, per, factors),
            jnp.pad(chosen_idio.reshape(owners, 1, per), ((0, 0), (0, 0), (0, factors - per))),
        ],
        axis=1,
    )
    arrived = lax.all_to_all(packed, BOX, 0, 0, tiled=True)
    reduced = jnp.sum(arrived, axis=0, keepdims=True)
    spread = jnp.broadcast_to(reduced, packed.shape)
    full = lax.all_to_all(spread, BOX, 0, 0, tiled=True)
    return full[:, :per, :].reshape(shocks, factors), full[:, per, :per].reshape(shocks)


def make_body(zh, xs):
    zsrc_t, group_t, pos_t, perm_in, perm_out, perm_x = layout(zh, xs)

    def on_device(coefs, lag_pattern, loadings, idiosyncratic, shocked):
        loadings, idiosyncratic = lax.ppermute((loadings, idiosyncratic), ALL, perm_in)
        coefs = lax.ppermute(coefs, ALL, perm_in)
        blk_dev = coefs.shape[0]
        lags = coefs.shape[1]
        block_size = coefs.shape[2]
        k = lax.axis_index("zh")
        zl = lax.axis_index("zl")
        y = lax.axis_index("y")
        c = lax.axis_index("c")
        x = lax.axis_index("x")
        owners = ZL * YS * CORE * xs
        mine = (jnp.asarray(zsrc_t)[k, zl, y, c, x] * YS + y) * CORE + c
        group_of_pos = jnp.asarray(group_t)[k]
        pos_of_group = jnp.asarray(pos_t)[k]
        n_blocks = owners * blk_dev
        capacity = min(blk_dev, max(1, blk_dev * lags // owners))
        shifted = jnp.stack([shocked] + [lax.ppermute(shocked, ALL, perm_x[j]) for j in range(1, xs)])
        shock_columns = shocked.shape[0]
        shocked = shifted[(x - k) % xs]
        local_rows = blk_dev * block_size
        row_ids = mine * local_rows + jnp.arange(local_rows, dtype=jnp.int32)
        pick_table = (shocked[:, None] == row_ids[None, :]).astype(jnp.float32)
        chosen = jnp.dot(
            pick_table, loadings, precision=lax.Precision.HIGHEST, preferred_element_type=jnp.float32
        )
        chosen_idio = jnp.dot(
            pick_table,
            idiosyncratic,
            precision=lax.Precision.HIGHEST,
            preferred_element_type=jnp.float32,
        )
        chosen, chosen_idio = gather_rows(chosen, chosen_idio, owners)
        scale = jnp.sqrt(jnp.sum(chosen * chosen, axis=1) + chosen_idio)
        impact = jnp.dot(
            loadings, chosen.T, precision=lax.Precision.HIGHEST, preferred_element_type=jnp.float32
        )
        impact = impact + pick_table.T * idiosyncratic[:, None]
        impact = impact / scale[None, :]
        present_response = impact.astype(jnp.bfloat16).reshape(blk_dev, block_size, shock_columns)
        squared_terms = present_response.astype(jnp.float32) ** 2
        my_lags = lax.dynamic_slice_in_dim(lag_pattern, mine * blk_dev, blk_dev, 0)
        flat_lags = my_lags.reshape(-1)
        all_blocks_ids = jnp.arange(n_blocks, dtype=jnp.int32)
        read_need = jnp.any(flat_lags[:, None] == all_blocks_ids[None, :], axis=0).astype(jnp.int32)
        read_need = read_need.reshape(owners, blk_dev)[group_of_pos]
        read_before = jnp.cumsum(read_need, axis=1) - read_need
        owner_base = jnp.arange(owners, dtype=jnp.int32)[:, None] * capacity
        slot_of_pos = (owner_base + read_before).reshape(-1)
        block_at = pos_of_group[flat_lags // blk_dev] * blk_dev + flat_lags % blk_dev
        take_index = slot_of_pos[block_at]
        reader_slots = lag_pattern.reshape(owners, blk_dev * lags)[group_of_pos]
        own_ids = mine * blk_dev + jnp.arange(blk_dev, dtype=jnp.int32)
        send_need = jnp.any(reader_slots[:, :, None] == own_ids[None, None, :], axis=1).astype(
            jnp.int32
        )
        send_before = jnp.cumsum(send_need, axis=1) - send_need
        cap_pos = jnp.arange(capacity, dtype=jnp.int32)
        routing_matrix = (
            (send_need[:, None, :] == 1) & (send_before[:, None, :] == cap_pos[None, :, None])
        ).astype(jnp.bfloat16)
        def one_step(step, carry):
            present_response, squared_terms = carry
            outgoing = jnp.einsum(
                "vwq,qfn->vwfn", routing_matrix, present_response, preferred_element_type=jnp.float32
            ).astype(jnp.bfloat16)
            arriving_response = lax.all_to_all(outgoing, BOX, split_axis=0, concat_axis=0, tiled=True)
            stacked = arriving_response.reshape(owners * capacity, block_size, shock_columns)
            lagged = jnp.take(stacked, take_index, axis=0).reshape(
                blk_dev, lags, block_size, shock_columns
            )
            product = jnp.einsum("rlij,rljs->ris", coefs, lagged, preferred_element_type=jnp.float32)
            present_response = product.astype(jnp.bfloat16)
            squared_terms = squared_terms + present_response.astype(jnp.float32) ** 2
            return present_response, squared_terms

        present_response, squared_terms = lax.fori_loop(
            0, HORIZONS - 1, one_step, (present_response, squared_terms)
        )
        partial = jnp.sum(squared_terms, axis=2)
        squared_terms = lax.ppermute(squared_terms, ALL, perm_out[0])
        parts = [lax.ppermute(partial, ALL, perm_out[j]) for j in range(xs)]
        totals = parts[0]
        for more in parts[1:]:
            totals = totals + more
        total_shocks = shock_columns * xs
        shares = total_shocks * squared_terms / (totals[:, :, None] + 1e-06)
        return shares.reshape(local_rows, shock_columns)

    return on_device


def solution(mesh):
    rows = mesh.shape["rows"]
    xs = mesh.shape["shock"]
    zh = rows // (ZL * YS * CORE)
    mesh5 = Mesh(mesh.devices.reshape(zh, ZL, YS, CORE, xs), ALL)
    rows_axes = ("zh", "zl", "y", "c")
    placed = (
        P(rows_axes, None, None, None),
        P(),
        P(rows_axes, None),
        P(rows_axes),
        P("x"),
    )
    return jax.shard_map(
        make_body(zh, xs), mesh=mesh5, in_specs=placed, out_specs=P(rows_axes, "x"), check_vma=False
    )
```

```python
import numpy as np
import jax
import jax.numpy as jnp
from jax import lax
from jax.sharding import Mesh
from jax.sharding import PartitionSpec as P
from jax.experimental import pallas as pl
from jax.experimental.pallas import tpu as pltpu

HORIZONS = 7
CORE = 2
YS = 4
ZL = 2
ALL = ("zh", "zl", "y", "c", "x")
BOX = ("zl", "y", "c", "x")


def layout(zh, xs):
    zs = zh * ZL
    flat = lambda k, zl, y, c, x: (((k * ZL + zl) * YS + y) * CORE + c) * xs + x
    group_of = np.zeros((zh, ZL * YS * CORE * xs), np.int32)
    pos_of = np.zeros((zh, zs * YS * CORE), np.int32)
    zsrc = np.zeros((zh, ZL, YS, CORE, xs), np.int32)
    perm_in, perm_out = [], []
    for k in range(zh):
        for zl in range(ZL):
            for y in range(YS):
                for c in range(CORE):
                    for x in range(xs):
                        d = x if c == 0 else xs - 1 - x
                        z = (ZL * k - d) % zs if zl == 0 else (ZL * k + 1 + d) % zs
                        zsrc[k, zl, y, c, x] = z
                        g = (z * YS + y) * CORE + c
                        pos = ((zl * YS + y) * CORE + c) * xs + x
                        group_of[k, pos] = g
                        pos_of[k, g] = pos
                        src = flat(z // ZL, z % ZL, y, c, x)
                        me = flat(k, zl, y, c, x)
                        perm_in.append((src, me))
                        perm_out.append((me, flat(z // ZL, z % ZL, y, c, k)))
    return zsrc, group_of, pos_of, perm_in, perm_out


def step_kernel(take_ref, send_ref, arrived_ref, coefs_ref, sq_ref, present_ref, sq_out_ref, out_ref):
    blk_dev, lags = coefs_ref.shape[0], coefs_ref.shape[1]
    for r in range(blk_dev):
        def body(l, acc):
            blk = arrived_ref[take_ref[r * lags + l]]
            return acc + jnp.dot(coefs_ref[r, l], blk, preferred_element_type=jnp.float32)
        acc = lax.fori_loop(0, lags, body, jnp.zeros(present_ref.shape[1:], jnp.float32))
        rounded = acc.astype(jnp.bfloat16)
        present_ref[r] = rounded
        wide = rounded.astype(jnp.float32)
        sq_out_ref[r] = sq_ref[r] + wide * wide

    def send(v, carry):
        out_ref[v] = present_ref[send_ref[v]]
        return carry
    lax.fori_loop(0, out_ref.shape[0], send, 0)

def step(take, send, arrived, coefs, squares):
    blk_dev, lags, bs, _ = coefs.shape
    cols = arrived.shape[2]
    n_out = send.shape[0]
    smem = pl.BlockSpec(memory_space=pltpu.SMEM)
    vmem = pl.BlockSpec(memory_space=pltpu.VMEM)
    return pl.pallas_call(
        step_kernel,
        out_shape=(
            jax.ShapeDtypeStruct((blk_dev, bs, cols), jnp.bfloat16),
            jax.ShapeDtypeStruct((blk_dev, bs, cols), jnp.float32),
            jax.ShapeDtypeStruct((n_out, bs, cols), jnp.bfloat16),
        ),
        in_specs=[smem, smem, vmem, vmem, vmem],
        out_specs=(vmem, vmem, vmem),
        input_output_aliases={4: 1},
    )(take, send, arrived, coefs, squares)


def gather_rows(chosen, chosen_idio, owners):
    shocks, factors = chosen.shape
    per = shocks // owners
    packed = jnp.concatenate(
        [
            chosen.reshape(owners, per, factors),
            jnp.pad(chosen_idio.reshape(owners, 1, per), ((0, 0), (0, 0), (0, factors - per))),
        ],
        axis=1,
    )
    arrived = lax.all_to_all(packed, BOX, 0, 0, tiled=True)
    reduced = jnp.sum(arrived, axis=0, keepdims=True)
    spread = jnp.broadcast_to(reduced, packed.shape)
    full = lax.all_to_all(spread, BOX, 0, 0, tiled=True)
    return full[:, :per, :].reshape(shocks, factors), full[:, per, :per].reshape(shocks)


def make_body(zh, xs):
    zsrc_t, group_t, pos_t, perm_in, perm_out = layout(zh, xs)

    def on_device(coefs, lag_pattern, loadings, idiosyncratic, shocked):
        loadings, idiosyncratic = lax.ppermute((loadings, idiosyncratic), ALL, perm_in)
        coefs = lax.ppermute(coefs, ALL, perm_in)
        blk_dev = coefs.shape[0]
        lags = coefs.shape[1]
        block_size = coefs.shape[2]
        k = lax.axis_index("zh")
        zl = lax.axis_index("zl")
        y = lax.axis_index("y")
        c = lax.axis_index("c")
        x = lax.axis_index("x")
        owners = ZL * YS * CORE * xs
        mine = (jnp.asarray(zsrc_t)[k, zl, y, c, x] * YS + y) * CORE + c
        group_of_pos = jnp.asarray(group_t)[k]
        pos_of_group = jnp.asarray(pos_t)[k]
        n_blocks = owners * blk_dev
        capacity = min(blk_dev, max(1, blk_dev * lags // owners))
        all_shocks = lax.all_gather(shocked, "x", axis=0, tiled=True)
        shock_columns = shocked.shape[0]
        shocked = lax.dynamic_slice_in_dim(all_shocks, k * shock_columns, shock_columns, 0)
        local_rows = blk_dev * block_size
        row_ids = mine * local_rows + jnp.arange(local_rows, dtype=jnp.int32)
        pick_table = (shocked[:, None] == row_ids[None, :]).astype(jnp.float32)
        chosen = jnp.dot(
            pick_table, loadings, precision=lax.Precision.HIGHEST, preferred_element_type=jnp.float32
        )
        chosen_idio = jnp.dot(
            pick_table,
            idiosyncratic,
            precision=lax.Precision.HIGHEST,
            preferred_element_type=jnp.float32,
        )
        chosen, chosen_idio = gather_rows(chosen, chosen_idio, owners)
        scale = jnp.sqrt(jnp.sum(chosen * chosen, axis=1) + chosen_idio)
        impact = jnp.dot(
            loadings, chosen.T, precision=lax.Precision.HIGHEST, preferred_element_type=jnp.float32
        )
        impact = impact + pick_table.T * idiosyncratic[:, None]
        impact = impact / scale[None, :]
        present_response = impact.astype(jnp.bfloat16).reshape(blk_dev, block_size, shock_columns)
        squared_terms = present_response.astype(jnp.float32) ** 2
        my_lags = lax.dynamic_slice_in_dim(lag_pattern, mine * blk_dev, blk_dev, 0)
        flat_lags = my_lags.reshape(-1)
        all_blocks_ids = jnp.arange(n_blocks, dtype=jnp.int32)
        read_need = jnp.any(flat_lags[:, None] == all_blocks_ids[None, :], axis=0).astype(jnp.int32)
        read_need = read_need.reshape(owners, blk_dev)[group_of_pos]
        read_before = jnp.cumsum(read_need, axis=1) - read_need
        owner_base = jnp.arange(owners, dtype=jnp.int32)[:, None] * capacity
        slot_of_pos = (owner_base + read_before).reshape(-1)
        block_at = pos_of_group[flat_lags // blk_dev] * blk_dev + flat_lags % blk_dev
        take_index = slot_of_pos[block_at]
        reader_slots = lag_pattern.reshape(owners, blk_dev * lags)[group_of_pos]
        own_ids = mine * blk_dev + jnp.arange(blk_dev, dtype=jnp.int32)
        send_need = jnp.any(reader_slots[:, :, None] == own_ids[None, None, :], axis=1).astype(
            jnp.int32
        )
        send_idx = jnp.argmax(send_need, axis=1).astype(jnp.int32)
        outgoing = jnp.take(present_response, send_idx, axis=0)
        for step_no in range(HORIZONS - 1):
            arriving_response = lax.all_to_all(outgoing, BOX, split_axis=0, concat_axis=0, tiled=True)
            present_response, squared_terms, outgoing = step(
                take_index, send_idx, arriving_response, coefs, squared_terms
            )
        partial = jnp.sum(squared_terms, axis=2)
        squared_terms, partial = lax.ppermute((squared_terms, partial), ALL, perm_out)
        totals = lax.psum(partial, "x")
        total_shocks = shock_columns * xs
        shares = total_shocks * squared_terms / (totals[:, :, None] + 1e-06)
        return shares.reshape(local_rows, shock_columns)

    return on_device


def solution(mesh):
    rows = mesh.shape["rows"]
    xs = mesh.shape["shock"]
    zh = rows // (ZL * YS * CORE)
    mesh5 = Mesh(mesh.devices.reshape(zh, ZL, YS, CORE, xs), ALL)
    rows_axes = ("zh", "zl", "y", "c")
    placed = (
        P(rows_axes, None, None, None),
        P(),
        P(rows_axes, None),
        P(rows_axes),
        P("x"),
    )
    return jax.shard_map(
        make_body(zh, xs), mesh=mesh5, in_specs=placed, out_specs=P(rows_axes, "x"), check_vma=False
    )
```

```python
import numpy as np
import jax
import jax.numpy as jnp
from jax import lax
from jax.sharding import Mesh
from jax.sharding import PartitionSpec as P
from jax.experimental import pallas as pl
from jax.experimental.pallas import tpu as pltpu

HORIZONS = 7
CORE = 2
YS = 4
ZL = 2
ALL = ("zh", "zl", "y", "c", "x")
BOX = ("zl", "y", "c", "x")


def layout(zh, xs):
    zs = zh * ZL
    flat = lambda k, zl, y, c, x: (((k * ZL + zl) * YS + y) * CORE + c) * xs + x
    group_of = np.zeros((zh, ZL * YS * CORE * xs), np.int32)
    pos_of = np.zeros((zh, zs * YS * CORE), np.int32)
    zsrc = np.zeros((zh, ZL, YS, CORE, xs), np.int32)
    perm_in, perm_out = [], []
    for k in range(zh):
        for zl in range(ZL):
            for y in range(YS):
                for c in range(CORE):
                    for x in range(xs):
                        d = x if c == 0 else xs - 1 - x
                        z = (ZL * k - d) % zs if zl == 0 else (ZL * k + 1 + d) % zs
                        zsrc[k, zl, y, c, x] = z
                        g = (z * YS + y) * CORE + c
                        pos = ((zl * YS + y) * CORE + c) * xs + x
                        group_of[k, pos] = g
                        pos_of[k, g] = pos
                        src = flat(z // ZL, z % ZL, y, c, x)
                        me = flat(k, zl, y, c, x)
                        perm_in.append((src, me))
                        perm_out.append((me, flat(z // ZL, z % ZL, y, c, k)))
    return zsrc, group_of, pos_of, perm_in, perm_out


def step_kernel(take_ref, send_ref, arrived_ref, coefs_ref, sq_ref, present_ref, sq_out_ref, out_hbm, lag_buf, sems):
    blk_dev, bs = coefs_ref.shape[0], coefs_ref.shape[1]
    lags = coefs_ref.shape[2] // bs
    for r in range(blk_dev):
        for l in range(lags):
            lag_buf[l * bs:(l + 1) * bs, :] = arrived_ref[take_ref[r * lags + l]]
        acc = jnp.dot(coefs_ref[r], lag_buf[...], preferred_element_type=jnp.float32)
        rounded = acc.astype(jnp.bfloat16)
        present_ref[r] = rounded
        wide = rounded.astype(jnp.float32)
        sq_out_ref[r] = sq_ref[r] + wide * wide
    copies = []
    for v in range(out_hbm.shape[0]):
        cp = pltpu.make_async_copy(present_ref.at[send_ref[v]], out_hbm.at[v], sems.at[v])
        cp.start()
        copies.append(cp)
    for cp in copies:
        cp.wait()


def step(take, send, arrived, coefs_wide, squares):
    blk_dev, bs, width = coefs_wide.shape
    cols = arrived.shape[2]
    n_out = send.shape[0]
    smem = pl.BlockSpec(memory_space=pltpu.SMEM)
    vmem = pl.BlockSpec(memory_space=pltpu.VMEM)
    hbm = pl.BlockSpec(memory_space=pl.ANY)
    return pl.pallas_call(
        step_kernel,
        out_shape=(
            jax.ShapeDtypeStruct((blk_dev, bs, cols), jnp.bfloat16),
            jax.ShapeDtypeStruct((blk_dev, bs, cols), jnp.float32),
            jax.ShapeDtypeStruct((n_out, bs, cols), jnp.bfloat16),
        ),
        in_specs=[smem, smem, vmem, vmem, vmem],
        out_specs=(vmem, vmem, hbm),
        scratch_shapes=[
            pltpu.VMEM((width, cols), jnp.bfloat16),
            pltpu.SemaphoreType.DMA((n_out,)),
        ],
        input_output_aliases={4: 1},
    )(take, send, arrived, coefs_wide, squares)


def gather_rows(chosen, chosen_idio, owners):
    shocks, factors = chosen.shape
    per = shocks // owners
    packed = jnp.concatenate(
        [
            chosen.reshape(owners, per, factors),
            jnp.pad(chosen_idio.reshape(owners, 1, per), ((0, 0), (0, 0), (0, factors - per))),
        ],
        axis=1,
    )
    arrived = lax.all_to_all(packed, BOX, 0, 0, tiled=True)
    reduced = jnp.sum(arrived, axis=0, keepdims=True)
    spread = jnp.broadcast_to(reduced, packed.shape)
    full = lax.all_to_all(spread, BOX, 0, 0, tiled=True)
    return full[:, :per, :].reshape(shocks, factors), full[:, per, :per].reshape(shocks)


def make_body(zh, xs):
    zsrc_t, group_t, pos_t, perm_in, perm_out = layout(zh, xs)

    def on_device(coefs, lag_pattern, loadings, idiosyncratic, shocked):
        loadings, idiosyncratic = lax.ppermute((loadings, idiosyncratic), ALL, perm_in)
        coefs = lax.ppermute(coefs, ALL, perm_in)
        blk_dev = coefs.shape[0]
        lags = coefs.shape[1]
        block_size = coefs.shape[2]
        k = lax.axis_index("zh")
        zl = lax.axis_index("zl")
        y = lax.axis_index("y")
        c = lax.axis_index("c")
        x = lax.axis_index("x")
        owners = ZL * YS * CORE * xs
        mine = (jnp.asarray(zsrc_t)[k, zl, y, c, x] * YS + y) * CORE + c
        group_of_pos = jnp.asarray(group_t)[k]
        pos_of_group = jnp.asarray(pos_t)[k]
        n_blocks = owners * blk_dev
        capacity = min(blk_dev, max(1, blk_dev * lags // owners))
        all_shocks = lax.all_gather(shocked, "x", axis=0, tiled=True)
        shock_columns = shocked.shape[0]
        shocked = lax.dynamic_slice_in_dim(all_shocks, k * shock_columns, shock_columns, 0)
        local_rows = blk_dev * block_size
        row_ids = mine * local_rows + jnp.arange(local_rows, dtype=jnp.int32)
        pick_table = (shocked[:, None] == row_ids[None, :]).astype(jnp.float32)
        chosen = jnp.dot(
            pick_table, loadings, precision=lax.Precision.HIGHEST, preferred_element_type=jnp.float32
        )
        chosen_idio = jnp.dot(
            pick_table,
            idiosyncratic,
            precision=lax.Precision.HIGHEST,
            preferred_element_type=jnp.float32,
        )
        chosen, chosen_idio = gather_rows(chosen, chosen_idio, owners)
        scale = jnp.sqrt(jnp.sum(chosen * chosen, axis=1) + chosen_idio)
        impact = jnp.dot(
            loadings, chosen.T, precision=lax.Precision.HIGHEST, preferred_element_type=jnp.float32
        )
        impact = impact + pick_table.T * idiosyncratic[:, None]
        impact = impact / scale[None, :]
        present_response = impact.astype(jnp.bfloat16).reshape(blk_dev, block_size, shock_columns)
        squared_terms = present_response.astype(jnp.float32) ** 2
        my_lags = lax.dynamic_slice_in_dim(lag_pattern, mine * blk_dev, blk_dev, 0)
        flat_lags = my_lags.reshape(-1)
        all_blocks_ids = jnp.arange(n_blocks, dtype=jnp.int32)
        read_need = jnp.any(flat_lags[:, None] == all_blocks_ids[None, :], axis=0).astype(jnp.int32)
        read_need = read_need.reshape(owners, blk_dev)[group_of_pos]
        read_before = jnp.cumsum(read_need, axis=1) - read_need
        owner_base = jnp.arange(owners, dtype=jnp.int32)[:, None] * capacity
        slot_of_pos = (owner_base + read_before).reshape(-1)
        block_at = pos_of_group[flat_lags // blk_dev] * blk_dev + flat_lags % blk_dev
        take_index = slot_of_pos[block_at]
        reader_slots = lag_pattern.reshape(owners, blk_dev * lags)[group_of_pos]
        own_ids = mine * blk_dev + jnp.arange(blk_dev, dtype=jnp.int32)
        send_need = jnp.any(reader_slots[:, :, None] == own_ids[None, None, :], axis=1).astype(
            jnp.int32
        )
        send_idx = jnp.argmax(send_need, axis=1).astype(jnp.int32)
        outgoing = jnp.take(present_response, send_idx, axis=0)
        coefs_wide = coefs.transpose(0, 2, 1, 3).reshape(blk_dev, block_size, lags * block_size)
        for step_no in range(HORIZONS - 1):
            arriving_response = lax.all_to_all(outgoing, BOX, split_axis=0, concat_axis=0, tiled=True)
            present_response, squared_terms, outgoing = step(
                take_index, send_idx, arriving_response, coefs_wide, squared_terms
            )
        partial = jnp.sum(squared_terms, axis=2)
        squared_terms, partial = lax.ppermute((squared_terms, partial), ALL, perm_out)
        totals = lax.psum(partial, "x")
        total_shocks = shock_columns * xs
        shares = total_shocks * squared_terms / (totals[:, :, None] + 1e-06)
        return shares.reshape(local_rows, shock_columns)

    return on_device


def solution(mesh):
    rows = mesh.shape["rows"]
    xs = mesh.shape["shock"]
    zh = rows // (ZL * YS * CORE)
    mesh5 = Mesh(mesh.devices.reshape(zh, ZL, YS, CORE, xs), ALL)
    rows_axes = ("zh", "zl", "y", "c")
    placed = (
        P(rows_axes, None, None, None),
        P(),
        P(rows_axes, None),
        P(rows_axes),
        P("x"),
    )
    return jax.shard_map(
        make_body(zh, xs), mesh=mesh5, in_specs=placed, out_specs=P(rows_axes, "x"), check_vma=False
    )
```

```python
import numpy as np
import jax
import jax.numpy as jnp
from jax import lax
from jax.sharding import Mesh
from jax.sharding import PartitionSpec as P
from jax.experimental import pallas as pl
from jax.experimental.pallas import tpu as pltpu

HORIZONS = 7
CORE = 2
YS = 4
ZL = 2
ALL = ("zh", "zl", "y", "c", "x")
BOX = ("zl", "y", "c", "x")


def layout(zh, xs):
    zs = zh * ZL
    flat = lambda k, zl, y, c, x: (((k * ZL + zl) * YS + y) * CORE + c) * xs + x
    group_of = np.zeros((zh, ZL * YS * CORE * xs), np.int32)
    pos_of = np.zeros((zh, zs * YS * CORE), np.int32)
    zsrc = np.zeros((zh, ZL, YS, CORE, xs), np.int32)
    perm_in, perm_out = [], []
    for k in range(zh):
        for zl in range(ZL):
            for y in range(YS):
                for c in range(CORE):
                    for x in range(xs):
                        d = x if c == 0 else xs - 1 - x
                        z = (ZL * k - d) % zs if zl == 0 else (ZL * k + 1 + d) % zs
                        zsrc[k, zl, y, c, x] = z
                        g = (z * YS + y) * CORE + c
                        pos = ((zl * YS + y) * CORE + c) * xs + x
                        group_of[k, pos] = g
                        pos_of[k, g] = pos
                        src = flat(z // ZL, z % ZL, y, c, x)
                        me = flat(k, zl, y, c, x)
                        perm_in.append((src, me))
                        perm_out.append((me, flat(z // ZL, z % ZL, y, c, k)))
    perm_x = [
        [(flat(k, zl, y, c, x), flat(k, zl, y, c, (x + j) % xs)) for k in range(zh) for zl in range(ZL)
         for y in range(YS) for c in range(CORE) for x in range(xs)]
        for j in range(xs)
    ]
    return zsrc, group_of, pos_of, perm_in, perm_out, perm_x


def step_kernel(take_ref, send_ref, arrived_ref, coefs_ref, sq_ref, present_ref, sq_out_ref, out_hbm, lag_buf, sems):
    blk_dev, bs = coefs_ref.shape[0], coefs_ref.shape[1]
    lags = coefs_ref.shape[2] // bs
    for r in range(blk_dev):
        for l in range(lags):
            lag_buf[l * bs:(l + 1) * bs, :] = arrived_ref[take_ref[r * lags + l]]
        acc = jnp.dot(coefs_ref[r], lag_buf[...], preferred_element_type=jnp.float32)
        rounded = acc.astype(jnp.bfloat16)
        present_ref[r] = rounded
        wide = rounded.astype(jnp.float32)
        sq_out_ref[r] = sq_ref[r] + wide * wide
    copies = []
    for v in range(out_hbm.shape[0]):
        cp = pltpu.make_async_copy(present_ref.at[send_ref[v]], out_hbm.at[v], sems.at[v])
        cp.start()
        copies.append(cp)
    for cp in copies:
        cp.wait()


def step(take, send, arrived, coefs_wide, squares):
    blk_dev, bs, width = coefs_wide.shape
    cols = arrived.shape[2]
    n_out = send.shape[0]
    smem = pl.BlockSpec(memory_space=pltpu.SMEM)
    vmem = pl.BlockSpec(memory_space=pltpu.VMEM)
    hbm = pl.BlockSpec(memory_space=pl.ANY)
    return pl.pallas_call(
        step_kernel,
        out_shape=(
            jax.ShapeDtypeStruct((blk_dev, bs, cols), jnp.bfloat16),
            jax.ShapeDtypeStruct((blk_dev, bs, cols), jnp.float32),
            jax.ShapeDtypeStruct((n_out, bs, cols), jnp.bfloat16),
        ),
        in_specs=[smem, smem, vmem, vmem, vmem],
        out_specs=(vmem, vmem, hbm),
        scratch_shapes=[
            pltpu.VMEM((width, cols), jnp.bfloat16),
            pltpu.SemaphoreType.DMA((n_out,)),
        ],
        input_output_aliases={4: 1},
    )(take, send, arrived, coefs_wide, squares)


def gather_rows(chosen, chosen_idio, owners):
    shocks, factors = chosen.shape
    per = shocks // owners
    packed = jnp.concatenate(
        [
            chosen.reshape(owners, per, factors),
            jnp.pad(chosen_idio.reshape(owners, 1, per), ((0, 0), (0, 0), (0, factors - per))),
        ],
        axis=1,
    )
    arrived = lax.all_to_all(packed, BOX, 0, 0, tiled=True)
    reduced = jnp.sum(arrived, axis=0, keepdims=True)
    spread = jnp.broadcast_to(reduced, packed.shape)
    full = lax.all_to_all(spread, BOX, 0, 0, tiled=True)
    return full[:, :per, :].reshape(shocks, factors), full[:, per, :per].reshape(shocks)


def make_body(zh, xs):
    zsrc_t, group_t, pos_t, perm_in, perm_out, perm_x = layout(zh, xs)

    def on_device(coefs, lag_pattern, loadings, idiosyncratic, shocked):
        loadings, idiosyncratic = lax.ppermute((loadings, idiosyncratic), ALL, perm_in)
        coefs = lax.ppermute(coefs, ALL, perm_in)
        blk_dev = coefs.shape[0]
        lags = coefs.shape[1]
        block_size = coefs.shape[2]
        k = lax.axis_index("zh")
        zl = lax.axis_index("zl")
        y = lax.axis_index("y")
        c = lax.axis_index("c")
        x = lax.axis_index("x")
        owners = ZL * YS * CORE * xs
        mine = (jnp.asarray(zsrc_t)[k, zl, y, c, x] * YS + y) * CORE + c
        group_of_pos = jnp.asarray(group_t)[k]
        pos_of_group = jnp.asarray(pos_t)[k]
        n_blocks = owners * blk_dev
        capacity = min(blk_dev, max(1, blk_dev * lags // owners))
        shifted = jnp.stack([shocked] + [lax.ppermute(shocked, ALL, perm_x[j]) for j in range(1, xs)])
        shock_columns = shocked.shape[0]
        shocked = shifted[(x - k) % xs]
        local_rows = blk_dev * block_size
        row_ids = mine * local_rows + jnp.arange(local_rows, dtype=jnp.int32)
        pick_table = (shocked[:, None] == row_ids[None, :]).astype(jnp.float32)
        chosen = jnp.dot(
            pick_table, loadings, precision=lax.Precision.HIGHEST, preferred_element_type=jnp.float32
        )
        chosen_idio = jnp.dot(
            pick_table,
            idiosyncratic,
            precision=lax.Precision.HIGHEST,
            preferred_element_type=jnp.float32,
        )
        chosen, chosen_idio = gather_rows(chosen, chosen_idio, owners)
        scale = jnp.sqrt(jnp.sum(chosen * chosen, axis=1) + chosen_idio)
        impact = jnp.dot(
            loadings, chosen.T, precision=lax.Precision.HIGHEST, preferred_element_type=jnp.float32
        )
        impact = impact + pick_table.T * idiosyncratic[:, None]
        impact = impact / scale[None, :]
        present_response = impact.astype(jnp.bfloat16).reshape(blk_dev, block_size, shock_columns)
        squared_terms = present_response.astype(jnp.float32) ** 2
        my_lags = lax.dynamic_slice_in_dim(lag_pattern, mine * blk_dev, blk_dev, 0)
        flat_lags = my_lags.reshape(-1)
        all_blocks_ids = jnp.arange(n_blocks, dtype=jnp.int32)
        read_need = jnp.any(flat_lags[:, None] == all_blocks_ids[None, :], axis=0).astype(jnp.int32)
        read_need = read_need.reshape(owners, blk_dev)[group_of_pos]
        read_before = jnp.cumsum(read_need, axis=1) - read_need
        owner_base = jnp.arange(owners, dtype=jnp.int32)[:, None] * capacity
        slot_of_pos = (owner_base + read_before).reshape(-1)
        block_at = pos_of_group[flat_lags // blk_dev] * blk_dev + flat_lags % blk_dev
        take_index = slot_of_pos[block_at]
        reader_slots = lag_pattern.reshape(owners, blk_dev * lags)[group_of_pos]
        own_ids = mine * blk_dev + jnp.arange(blk_dev, dtype=jnp.int32)
        send_need = jnp.any(reader_slots[:, :, None] == own_ids[None, None, :], axis=1).astype(
            jnp.int32
        )
        send_idx = jnp.argmax(send_need, axis=1).astype(jnp.int32)
        outgoing = jnp.take(present_response, send_idx, axis=0)
        coefs_wide = coefs.transpose(0, 2, 1, 3).reshape(blk_dev, block_size, lags * block_size)
        for step_no in range(HORIZONS - 1):
            arriving_response = lax.all_to_all(outgoing, BOX, split_axis=0, concat_axis=0, tiled=True)
            present_response, squared_terms, outgoing = step(
                take_index, send_idx, arriving_response, coefs_wide, squared_terms
            )
        partial = jnp.sum(squared_terms, axis=2)
        squared_terms, partial = lax.ppermute((squared_terms, partial), ALL, perm_out)
        totals = lax.psum(partial, "x")
        total_shocks = shock_columns * xs
        shares = total_shocks * squared_terms / (totals[:, :, None] + 1e-06)
        return shares.reshape(local_rows, shock_columns)

    return on_device


def solution(mesh):
    rows = mesh.shape["rows"]
    xs = mesh.shape["shock"]
    zh = rows // (ZL * YS * CORE)
    mesh5 = Mesh(mesh.devices.reshape(zh, ZL, YS, CORE, xs), ALL)
    rows_axes = ("zh", "zl", "y", "c")
    placed = (
        P(rows_axes, None, None, None),
        P(),
        P(rows_axes, None),
        P(rows_axes),
        P("x"),
    )
    return jax.shard_map(
        make_body(zh, xs), mesh=mesh5, in_specs=placed, out_specs=P(rows_axes, "x"), check_vma=False
    )
```

```python
import numpy as np
import jax
import jax.numpy as jnp
from jax import lax
from jax.sharding import Mesh
from jax.sharding import PartitionSpec as P
from jax.experimental import pallas as pl
from jax.experimental.pallas import tpu as pltpu

HORIZONS = 7
CORE = 2
YS = 4
ZL = 2
ALL = ("zh", "zl", "y", "c", "x")
BOX = ("zl", "y", "c", "x")


def layout(zh, xs):
    zs = zh * ZL
    flat = lambda k, zl, y, c, x: (((k * ZL + zl) * YS + y) * CORE + c) * xs + x
    group_of = np.zeros((zh, ZL * YS * CORE * xs), np.int32)
    pos_of = np.zeros((zh, zs * YS * CORE), np.int32)
    zsrc = np.zeros((zh, ZL, YS, CORE, xs), np.int32)
    perm_in, perm_out = [], []
    for k in range(zh):
        for zl in range(ZL):
            for y in range(YS):
                for c in range(CORE):
                    for x in range(xs):
                        d = x if c == 0 else xs - 1 - x
                        z = (ZL * k - d) % zs if zl == 0 else (ZL * k + 1 + d) % zs
                        zsrc[k, zl, y, c, x] = z
                        g = (z * YS + y) * CORE + c
                        pos = ((zl * YS + y) * CORE + c) * xs + x
                        group_of[k, pos] = g
                        pos_of[k, g] = pos
                        src = flat(z // ZL, z % ZL, y, c, x)
                        me = flat(k, zl, y, c, x)
                        perm_in.append((src, me))
                        perm_out.append((me, flat(z // ZL, z % ZL, y, c, k)))
    perm_x = [
        [(flat(k, zl, y, c, x), flat(k, zl, y, c, (x + j) % xs)) for k in range(zh) for zl in range(ZL)
         for y in range(YS) for c in range(CORE) for x in range(xs)]
        for j in range(xs)
    ]
    return zsrc, group_of, pos_of, perm_in, perm_out, perm_x


def step_kernel(take_ref, send_ref, arrived_ref, coefs_ref, sq_ref, present_ref, sq_out_ref, out_hbm, lag_buf, sems):
    blk_dev, bs = coefs_ref.shape[0], coefs_ref.shape[1]
    lags = coefs_ref.shape[2] // bs
    for r in range(blk_dev):
        for l in range(lags):
            lag_buf[l * bs:(l + 1) * bs, :] = arrived_ref[take_ref[r * lags + l]]
        acc = jnp.dot(coefs_ref[r], lag_buf[...], preferred_element_type=jnp.float32)
        rounded = acc.astype(jnp.bfloat16)
        present_ref[r] = rounded
        wide = rounded.astype(jnp.float32)
        sq_out_ref[r] = sq_ref[r] + wide * wide
    copies = []
    for v in range(out_hbm.shape[0]):
        cp = pltpu.make_async_copy(present_ref.at[send_ref[v]], out_hbm.at[v], sems.at[v])
        cp.start()
        copies.append(cp)
    for cp in copies:
        cp.wait()


def step(take, send, arrived, coefs_wide, squares):
    blk_dev, bs, width = coefs_wide.shape
    cols = arrived.shape[2]
    n_out = send.shape[0]
    smem = pl.BlockSpec(memory_space=pltpu.SMEM)
    vmem = pl.BlockSpec(memory_space=pltpu.VMEM)
    hbm = pl.BlockSpec(memory_space=pl.ANY)
    return pl.pallas_call(
        step_kernel,
        out_shape=(
            jax.ShapeDtypeStruct((blk_dev, bs, cols), jnp.bfloat16),
            jax.ShapeDtypeStruct((blk_dev, bs, cols), jnp.float32),
            jax.ShapeDtypeStruct((n_out, bs, cols), jnp.bfloat16),
        ),
        in_specs=[smem, smem, vmem, vmem, vmem],
        out_specs=(vmem, vmem, hbm),
        scratch_shapes=[
            pltpu.VMEM((width, cols), jnp.bfloat16),
            pltpu.SemaphoreType.DMA((n_out,)),
        ],
        input_output_aliases={4: 1},
    )(take, send, arrived, coefs_wide, squares)


def gather_rows(chosen, chosen_idio, owners):
    shocks, factors = chosen.shape
    per = shocks // owners
    packed = jnp.concatenate(
        [
            chosen.reshape(owners, per, factors),
            jnp.pad(chosen_idio.reshape(owners, 1, per), ((0, 0), (0, 0), (0, factors - per))),
        ],
        axis=1,
    )
    arrived = lax.all_to_all(packed, BOX, 0, 0, tiled=True)
    reduced = jnp.sum(arrived, axis=0, keepdims=True)
    spread = jnp.broadcast_to(reduced, packed.shape)
    full = lax.all_to_all(spread, BOX, 0, 0, tiled=True)
    return full[:, :per, :].reshape(shocks, factors), full[:, per, :per].reshape(shocks)


def make_body(zh, xs):
    zsrc_t, group_t, pos_t, perm_in, perm_out, perm_x = layout(zh, xs)

    def on_device(coefs, lag_pattern, loadings, idiosyncratic, shocked):
        loadings, idiosyncratic = lax.ppermute((loadings, idiosyncratic), ALL, perm_in)
        blk_dev = coefs.shape[0]
        lags = coefs.shape[1]
        block_size = coefs.shape[2]
        coefs_wide = coefs.transpose(0, 2, 1, 3).reshape(blk_dev, block_size, lags * block_size)
        coefs_wide = lax.ppermute(coefs_wide, ALL, perm_in)
        k = lax.axis_index("zh")
        zl = lax.axis_index("zl")
        y = lax.axis_index("y")
        c = lax.axis_index("c")
        x = lax.axis_index("x")
        owners = ZL * YS * CORE * xs
        mine = (jnp.asarray(zsrc_t)[k, zl, y, c, x] * YS + y) * CORE + c
        group_of_pos = jnp.asarray(group_t)[k]
        pos_of_group = jnp.asarray(pos_t)[k]
        n_blocks = owners * blk_dev
        capacity = min(blk_dev, max(1, blk_dev * lags // owners))
        shifted = jnp.stack([shocked] + [lax.ppermute(shocked, ALL, perm_x[j]) for j in range(1, xs)])
        shock_columns = shocked.shape[0]
        shocked = shifted[(x - k) % xs]
        local_rows = blk_dev * block_size
        row_ids = mine * local_rows + jnp.arange(local_rows, dtype=jnp.int32)
        pick_table = (shocked[:, None] == row_ids[None, :]).astype(jnp.float32)
        chosen = jnp.dot(
            pick_table, loadings, precision=lax.Precision.HIGHEST, preferred_element_type=jnp.float32
        )
        chosen_idio = jnp.dot(
            pick_table,
            idiosyncratic,
            precision=lax.Precision.HIGHEST,
            preferred_element_type=jnp.float32,
        )
        chosen, chosen_idio = gather_rows(chosen, chosen_idio, owners)
        scale = jnp.sqrt(jnp.sum(chosen * chosen, axis=1) + chosen_idio)
        impact = jnp.dot(
            loadings, chosen.T, precision=lax.Precision.HIGHEST, preferred_element_type=jnp.float32
        )
        impact = impact + pick_table.T * idiosyncratic[:, None]
        impact = impact / scale[None, :]
        present_response = impact.astype(jnp.bfloat16).reshape(blk_dev, block_size, shock_columns)
        squared_terms = present_response.astype(jnp.float32) ** 2
        my_lags = lax.dynamic_slice_in_dim(lag_pattern, mine * blk_dev, blk_dev, 0)
        flat_lags = my_lags.reshape(-1)
        all_blocks_ids = jnp.arange(n_blocks, dtype=jnp.int32)
        read_need = jnp.any(flat_lags[:, None] == all_blocks_ids[None, :], axis=0).astype(jnp.int32)
        read_need = read_need.reshape(owners, blk_dev)[group_of_pos]
        read_before = jnp.cumsum(read_need, axis=1) - read_need
        owner_base = jnp.arange(owners, dtype=jnp.int32)[:, None] * capacity
        slot_of_pos = (owner_base + read_before).reshape(-1)
        block_at = pos_of_group[flat_lags // blk_dev] * blk_dev + flat_lags % blk_dev
        take_index = slot_of_pos[block_at]
        reader_slots = lag_pattern.reshape(owners, blk_dev * lags)[group_of_pos]
        own_ids = mine * blk_dev + jnp.arange(blk_dev, dtype=jnp.int32)
        send_need = jnp.any(reader_slots[:, :, None] == own_ids[None, None, :], axis=1).astype(
            jnp.int32
        )
        send_idx = jnp.argmax(send_need, axis=1).astype(jnp.int32)
        outgoing = jnp.take(present_response, send_idx, axis=0)
        for step_no in range(HORIZONS - 1):
            arriving_response = lax.all_to_all(outgoing, BOX, split_axis=0, concat_axis=0, tiled=True)
            present_response, squared_terms, outgoing = step(
                take_index, send_idx, arriving_response, coefs_wide, squared_terms
            )
        partial = jnp.sum(squared_terms, axis=2)
        squared_terms, partial = lax.ppermute((squared_terms, partial), ALL, perm_out)
        totals = lax.psum(partial, "x")
        total_shocks = shock_columns * xs
        shares = total_shocks * squared_terms / (totals[:, :, None] + 1e-06)
        return shares.reshape(local_rows, shock_columns)

    return on_device


def solution(mesh):
    rows = mesh.shape["rows"]
    xs = mesh.shape["shock"]
    zh = rows // (ZL * YS * CORE)
    mesh5 = Mesh(mesh.devices.reshape(zh, ZL, YS, CORE, xs), ALL)
    rows_axes = ("zh", "zl", "y", "c")
    placed = (
        P(rows_axes, None, None, None),
        P(),
        P(rows_axes, None),
        P(rows_axes),
        P("x"),
    )
    return jax.shard_map(
        make_body(zh, xs), mesh=mesh5, in_specs=placed, out_specs=P(rows_axes, "x"), check_vma=False
    )
```

```python
import numpy as np
import jax
import jax.numpy as jnp
from jax import lax
from jax.sharding import Mesh
from jax.sharding import PartitionSpec as P
from jax.experimental import pallas as pl
from jax.experimental.pallas import tpu as pltpu

HORIZONS = 7
CORE = 2
YS = 4
ZL = 2
ALL = ("zh", "zl", "y", "c", "x")
BOX = ("zl", "y", "c", "x")


def layout(zh, xs):
    zs = zh * ZL
    flat = lambda k, zl, y, c, x: (((k * ZL + zl) * YS + y) * CORE + c) * xs + x
    group_of = np.zeros((zh, ZL * YS * CORE * xs), np.int32)
    pos_of = np.zeros((zh, zs * YS * CORE), np.int32)
    zsrc = np.zeros((zh, ZL, YS, CORE, xs), np.int32)
    perm_in, perm_out = [], []
    for k in range(zh):
        for zl in range(ZL):
            for y in range(YS):
                for c in range(CORE):
                    for x in range(xs):
                        d = x if c == 0 else xs - 1 - x
                        z = (ZL * k - d) % zs if zl == 0 else (ZL * k + 1 + d) % zs
                        zsrc[k, zl, y, c, x] = z
                        g = (z * YS + y) * CORE + c
                        pos = ((zl * YS + y) * CORE + c) * xs + x
                        group_of[k, pos] = g
                        pos_of[k, g] = pos
                        src = flat(z // ZL, z % ZL, y, c, x)
                        me = flat(k, zl, y, c, x)
                        perm_in.append((src, me))
                        perm_out.append((me, flat(z // ZL, z % ZL, y, c, k)))
    perm_x = [
        [(flat(k, zl, y, c, x), flat(k, zl, y, c, (x + j) % xs)) for k in range(zh) for zl in range(ZL)
         for y in range(YS) for c in range(CORE) for x in range(xs)]
        for j in range(xs)
    ]
    return zsrc, group_of, pos_of, perm_in, perm_out, perm_x


def step_kernel(take_ref, send_ref, arrived_ref, coefs_ref, sq_ref, present_ref, sq_out_ref, out_hbm, lag_buf, sems):
    blk_dev, bs = coefs_ref.shape[0], coefs_ref.shape[1]
    lags = coefs_ref.shape[2] // bs
    for r in range(blk_dev):
        for l in range(lags):
            lag_buf[l * bs:(l + 1) * bs, :] = arrived_ref[take_ref[r * lags + l]]
        acc = jnp.dot(coefs_ref[r], lag_buf[...], preferred_element_type=jnp.float32)
        rounded = acc.astype(jnp.bfloat16)
        present_ref[r] = rounded
        wide = rounded.astype(jnp.float32)
        sq_out_ref[r] = sq_ref[r] + wide * wide
    copies = []
    for v in range(out_hbm.shape[0]):
        cp = pltpu.make_async_copy(present_ref.at[send_ref[v]], out_hbm.at[v], sems.at[v])
        cp.start()
        copies.append(cp)
    for cp in copies:
        cp.wait()


def step(take, send, arrived, coefs_wide, squares):
    blk_dev, bs, width = coefs_wide.shape
    cols = arrived.shape[2]
    n_out = send.shape[0]
    smem = pl.BlockSpec(memory_space=pltpu.SMEM)
    vmem = pl.BlockSpec(memory_space=pltpu.VMEM)
    hbm = pl.BlockSpec(memory_space=pl.ANY)
    return pl.pallas_call(
        step_kernel,
        out_shape=(
            jax.ShapeDtypeStruct((blk_dev, bs, cols), jnp.bfloat16),
            jax.ShapeDtypeStruct((blk_dev, bs, cols), jnp.float32),
            jax.ShapeDtypeStruct((n_out, bs, cols), jnp.bfloat16),
        ),
        in_specs=[smem, smem, vmem, vmem, vmem],
        out_specs=(vmem, vmem, hbm),
        scratch_shapes=[
            pltpu.VMEM((width, cols), jnp.bfloat16),
            pltpu.SemaphoreType.DMA((n_out,)),
        ],
        input_output_aliases={4: 1},
    )(take, send, arrived, coefs_wide, squares)


def gather_rows(chosen, chosen_idio, owners):
    shocks, factors = chosen.shape
    per = shocks // owners
    packed = jnp.concatenate(
        [
            chosen.reshape(owners, per, factors),
            jnp.pad(chosen_idio.reshape(owners, 1, per), ((0, 0), (0, 0), (0, factors - per))),
        ],
        axis=1,
    )
    arrived = lax.all_to_all(packed, BOX, 0, 0, tiled=True)
    reduced = jnp.sum(arrived, axis=0, keepdims=True)
    spread = jnp.broadcast_to(reduced, packed.shape)
    full = lax.all_to_all(spread, BOX, 0, 0, tiled=True)
    return full[:, :per, :].reshape(shocks, factors), full[:, per, :per].reshape(shocks)


def make_body(zh, xs):
    zsrc_t, group_t, pos_t, perm_in, perm_out, perm_x = layout(zh, xs)

    def on_device(coefs, lag_pattern, loadings, idiosyncratic, shocked):
        loadings, idiosyncratic = lax.ppermute((loadings, idiosyncratic), ALL, perm_in)
        coefs = lax.ppermute(coefs, ALL, perm_in)
        blk_dev = coefs.shape[0]
        lags = coefs.shape[1]
        block_size = coefs.shape[2]
        k = lax.axis_index("zh")
        zl = lax.axis_index("zl")
        y = lax.axis_index("y")
        c = lax.axis_index("c")
        x = lax.axis_index("x")
        owners = ZL * YS * CORE * xs
        mine = (jnp.asarray(zsrc_t)[k, zl, y, c, x] * YS + y) * CORE + c
        group_of_pos = jnp.asarray(group_t)[k]
        pos_of_group = jnp.asarray(pos_t)[k]
        n_blocks = owners * blk_dev
        capacity = min(blk_dev, max(1, blk_dev * lags // owners))
        shifted = jnp.stack([shocked] + [lax.ppermute(shocked, ALL, perm_x[j]) for j in range(1, xs)])
        shock_columns = shocked.shape[0]
        shocked = shifted[(x - k) % xs]
        local_rows = blk_dev * block_size
        row_ids = mine * local_rows + jnp.arange(local_rows, dtype=jnp.int32)
        pick_table = (shocked[:, None] == row_ids[None, :]).astype(jnp.float32)
        chosen = jnp.dot(
            pick_table, loadings, precision=lax.Precision.HIGHEST, preferred_element_type=jnp.float32
        )
        chosen_idio = jnp.dot(
            pick_table,
            idiosyncratic,
            precision=lax.Precision.HIGHEST,
            preferred_element_type=jnp.float32,
        )
        chosen, chosen_idio = gather_rows(chosen, chosen_idio, owners)
        scale = jnp.sqrt(jnp.sum(chosen * chosen, axis=1) + chosen_idio)
        impact = jnp.dot(
            loadings, chosen.T, precision=lax.Precision.HIGHEST, preferred_element_type=jnp.float32
        )
        impact = impact + pick_table.T * idiosyncratic[:, None]
        impact = impact / scale[None, :]
        present_response = impact.astype(jnp.bfloat16).reshape(blk_dev, block_size, shock_columns)
        squared_terms = present_response.astype(jnp.float32) ** 2
        my_lags = lax.dynamic_slice_in_dim(lag_pattern, mine * blk_dev, blk_dev, 0)
        flat_lags = my_lags.reshape(-1)
        all_blocks_ids = jnp.arange(n_blocks, dtype=jnp.int32)
        read_need = jnp.any(flat_lags[:, None] == all_blocks_ids[None, :], axis=0).astype(jnp.int32)
        read_need = read_need.reshape(owners, blk_dev)[group_of_pos]
        read_before = jnp.cumsum(read_need, axis=1) - read_need
        owner_base = jnp.arange(owners, dtype=jnp.int32)[:, None] * capacity
        slot_of_pos = (owner_base + read_before).reshape(-1)
        block_at = pos_of_group[flat_lags // blk_dev] * blk_dev + flat_lags % blk_dev
        take_index = slot_of_pos[block_at]
        reader_slots = lag_pattern.reshape(owners, blk_dev * lags)[group_of_pos]
        own_ids = mine * blk_dev + jnp.arange(blk_dev, dtype=jnp.int32)
        send_need = jnp.any(reader_slots[:, :, None] == own_ids[None, None, :], axis=1).astype(
            jnp.int32
        )
        send_idx = jnp.argmax(send_need, axis=1).astype(jnp.int32)
        outgoing = jnp.take(present_response, send_idx, axis=0)
        coefs_wide = coefs.transpose(0, 2, 1, 3).reshape(blk_dev, block_size, lags * block_size)
        for step_no in range(HORIZONS - 2):
            arriving_response = lax.all_to_all(outgoing, BOX, split_axis=0, concat_axis=0, tiled=True)
            present_response, squared_terms, outgoing = step(
                take_index, send_idx, arriving_response, coefs_wide, squared_terms
            )
        earlier_squares = lax.ppermute(squared_terms, ALL, perm_out)
        arriving_response = lax.all_to_all(outgoing, BOX, split_axis=0, concat_axis=0, tiled=True)
        present_response, squared_terms, _ = step(
            take_index, send_idx, arriving_response, coefs_wide, squared_terms
        )
        partial = jnp.sum(squared_terms, axis=2)
        last_response, partial = lax.ppermute((present_response, partial), ALL, perm_out)
        wide_last = last_response.astype(jnp.float32)
        squared_terms = earlier_squares + wide_last * wide_last
        totals = lax.psum(partial, "x")
        total_shocks = shock_columns * xs
        shares = total_shocks * squared_terms / (totals[:, :, None] + 1e-06)
        return shares.reshape(local_rows, shock_columns)

    return on_device


def solution(mesh):
    rows = mesh.shape["rows"]
    xs = mesh.shape["shock"]
    zh = rows // (ZL * YS * CORE)
    mesh5 = Mesh(mesh.devices.reshape(zh, ZL, YS, CORE, xs), ALL)
    rows_axes = ("zh", "zl", "y", "c")
    placed = (
        P(rows_axes, None, None, None),
        P(),
        P(rows_axes, None),
        P(rows_axes),
        P("x"),
    )
    return jax.shard_map(
        make_body(zh, xs), mesh=mesh5, in_specs=placed, out_specs=P(rows_axes, "x"), check_vma=False
    )
```

```python
import numpy as np
import jax
import jax.numpy as jnp
from jax import lax
from jax.sharding import Mesh
from jax.sharding import PartitionSpec as P
from jax.experimental import pallas as pl
from jax.experimental.pallas import tpu as pltpu

HORIZONS = 7
CORE = 2
YS = 4
ZL = 2
ALL = ("zh", "zl", "y", "c", "x")
BOX = ("zl", "y", "c", "x")


def layout(zh, xs):
    zs = zh * ZL
    flat = lambda k, zl, y, c, x: (((k * ZL + zl) * YS + y) * CORE + c) * xs + x
    group_of = np.zeros((zh, ZL * YS * CORE * xs), np.int32)
    pos_of = np.zeros((zh, zs * YS * CORE), np.int32)
    zsrc = np.zeros((zh, ZL, YS, CORE, xs), np.int32)
    perm_in, perm_out = [], []
    for k in range(zh):
        for zl in range(ZL):
            for y in range(YS):
                for c in range(CORE):
                    for x in range(xs):
                        d = x if c == 0 else xs - 1 - x
                        z = (ZL * k - d) % zs if zl == 0 else (ZL * k + 1 + d) % zs
                        zsrc[k, zl, y, c, x] = z
                        g = (z * YS + y) * CORE + c
                        pos = ((zl * YS + y) * CORE + c) * xs + x
                        group_of[k, pos] = g
                        pos_of[k, g] = pos
                        src = flat(z // ZL, z % ZL, y, c, x)
                        me = flat(k, zl, y, c, x)
                        perm_in.append((src, me))
                        perm_out.append((me, flat(z // ZL, z % ZL, y, c, k)))
    perm_x = [
        [(flat(k, zl, y, c, x), flat(k, zl, y, c, (x + j) % xs)) for k in range(zh) for zl in range(ZL)
         for y in range(YS) for c in range(CORE) for x in range(xs)]
        for j in range(xs)
    ]
    return zsrc, group_of, pos_of, perm_in, perm_out, perm_x


def step_kernel(take_ref, send_ref, arrived_ref, coefs_ref, sq_ref, present_ref, sq_out_ref, out_hbm, lag_buf, sems):
    blk_dev, bs = coefs_ref.shape[0], coefs_ref.shape[1]
    lags = coefs_ref.shape[2] // bs
    for r in range(blk_dev):
        for l in range(lags):
            lag_buf[l * bs:(l + 1) * bs, :] = arrived_ref[take_ref[r * lags + l]]
        acc = jnp.dot(coefs_ref[r], lag_buf[...], preferred_element_type=jnp.float32)
        rounded = acc.astype(jnp.bfloat16)
        present_ref[r] = rounded
        wide = rounded.astype(jnp.float32)
        sq_out_ref[r] = sq_ref[r] + wide * wide
    copies = []
    for v in range(out_hbm.shape[0]):
        cp = pltpu.make_async_copy(present_ref.at[send_ref[v]], out_hbm.at[v], sems.at[v])
        cp.start()
        copies.append(cp)
    for cp in copies:
        cp.wait()


def step(take, send, arrived, coefs_wide, squares):
    blk_dev, bs, width = coefs_wide.shape
    cols = arrived.shape[2]
    n_out = send.shape[0]
    smem = pl.BlockSpec(memory_space=pltpu.SMEM)
    vmem = pl.BlockSpec(memory_space=pltpu.VMEM)
    hbm = pl.BlockSpec(memory_space=pl.ANY)
    return pl.pallas_call(
        step_kernel,
        out_shape=(
            jax.ShapeDtypeStruct((blk_dev, bs, cols), jnp.bfloat16),
            jax.ShapeDtypeStruct((blk_dev, bs, cols), jnp.float32),
            jax.ShapeDtypeStruct((n_out, bs, cols), jnp.bfloat16),
        ),
        in_specs=[smem, smem, vmem, vmem, vmem],
        out_specs=(vmem, vmem, hbm),
        scratch_shapes=[
            pltpu.VMEM((width, cols), jnp.bfloat16),
            pltpu.SemaphoreType.DMA((n_out,)),
        ],
        input_output_aliases={4: 1},
    )(take, send, arrived, coefs_wide, squares)


def gather_rows(chosen, chosen_idio, owners):
    shocks, factors = chosen.shape
    per = shocks // owners
    packed = jnp.concatenate(
        [
            chosen.reshape(owners, per, factors),
            jnp.pad(chosen_idio.reshape(owners, 1, per), ((0, 0), (0, 0), (0, factors - per))),
        ],
        axis=1,
    )
    arrived = lax.all_to_all(packed, BOX, 0, 0, tiled=True)
    reduced = jnp.sum(arrived, axis=0, keepdims=True)
    spread = jnp.broadcast_to(reduced, packed.shape)
    full = lax.all_to_all(spread, BOX, 0, 0, tiled=True)
    return full[:, :per, :].reshape(shocks, factors), full[:, per, :per].reshape(shocks)


def make_body(zh, xs):
    zsrc_t, group_t, pos_t, perm_in, perm_out, perm_x = layout(zh, xs)

    def on_device(coefs, lag_pattern, loadings, idiosyncratic, shocked):
        loadings, idiosyncratic = lax.ppermute((loadings, idiosyncratic), ALL, perm_in)
        coefs = lax.ppermute(coefs, ALL, perm_in)
        blk_dev = coefs.shape[0]
        lags = coefs.shape[1]
        block_size = coefs.shape[2]
        k = lax.axis_index("zh")
        zl = lax.axis_index("zl")
        y = lax.axis_index("y")
        c = lax.axis_index("c")
        x = lax.axis_index("x")
        owners = ZL * YS * CORE * xs
        mine = (jnp.asarray(zsrc_t)[k, zl, y, c, x] * YS + y) * CORE + c
        group_of_pos = jnp.asarray(group_t)[k]
        pos_of_group = jnp.asarray(pos_t)[k]
        n_blocks = owners * blk_dev
        capacity = min(blk_dev, max(1, blk_dev * lags // owners))
        shifted = jnp.stack([shocked] + [lax.ppermute(shocked, ALL, perm_x[j]) for j in range(1, xs)])
        shock_columns = shocked.shape[0]
        shocked = shifted[(x - k) % xs]
        local_rows = blk_dev * block_size
        row_ids = mine * local_rows + jnp.arange(local_rows, dtype=jnp.int32)
        pick_table = (shocked[:, None] == row_ids[None, :]).astype(jnp.float32)
        chosen = jnp.dot(
            pick_table, loadings, precision=lax.Precision.HIGHEST, preferred_element_type=jnp.float32
        )
        chosen_idio = jnp.dot(
            pick_table,
            idiosyncratic,
            precision=lax.Precision.HIGHEST,
            preferred_element_type=jnp.float32,
        )
        chosen, chosen_idio = gather_rows(chosen, chosen_idio, owners)
        scale = jnp.sqrt(jnp.sum(chosen * chosen, axis=1) + chosen_idio)
        impact = jnp.dot(
            loadings, chosen.T, precision=lax.Precision.HIGHEST, preferred_element_type=jnp.float32
        )
        impact = impact + pick_table.T * idiosyncratic[:, None]
        impact = impact / scale[None, :]
        present_response = impact.astype(jnp.bfloat16).reshape(blk_dev, block_size, shock_columns)
        squared_terms = present_response.astype(jnp.float32) ** 2
        my_lags = lax.dynamic_slice_in_dim(lag_pattern, mine * blk_dev, blk_dev, 0)
        flat_lags = my_lags.reshape(-1)
        all_blocks_ids = jnp.arange(n_blocks, dtype=jnp.int32)
        read_need = jnp.any(flat_lags[:, None] == all_blocks_ids[None, :], axis=0).astype(jnp.int32)
        read_need = read_need.reshape(owners, blk_dev)[group_of_pos]
        read_before = jnp.cumsum(read_need, axis=1) - read_need
        owner_base = jnp.arange(owners, dtype=jnp.int32)[:, None] * capacity
        slot_of_pos = (owner_base + read_before).reshape(-1)
        block_at = pos_of_group[flat_lags // blk_dev] * blk_dev + flat_lags % blk_dev
        take_index = slot_of_pos[block_at]
        reader_slots = lag_pattern.reshape(owners, blk_dev * lags)[group_of_pos]
        own_ids = mine * blk_dev + jnp.arange(blk_dev, dtype=jnp.int32)
        send_need = jnp.any(reader_slots[:, :, None] == own_ids[None, None, :], axis=1).astype(
            jnp.int32
        )
        send_idx = jnp.argmax(send_need, axis=1).astype(jnp.int32)
        outgoing = jnp.take(present_response, send_idx, axis=0)
        coefs_wide = coefs.transpose(0, 2, 1, 3).reshape(blk_dev, block_size, lags * block_size)
        for step_no in range(HORIZONS - 2):
            arriving_response = lax.all_to_all(outgoing, BOX, split_axis=0, concat_axis=0, tiled=True)
            present_response, squared_terms, outgoing = step(
                take_index, send_idx, arriving_response, coefs_wide, squared_terms
            )
        earlier_squares = lax.ppermute(squared_terms, ALL, perm_out)
        arriving_response = lax.all_to_all(outgoing, BOX, split_axis=0, concat_axis=0, tiled=True)
        present_response, squared_terms, _ = step(
            take_index, send_idx, arriving_response, coefs_wide, squared_terms
        )
        partial = jnp.sum(squared_terms, axis=2)
        last_response, partial = lax.ppermute((present_response, partial), ALL, perm_out)
        wide_last = last_response.astype(jnp.float32)
        squared_terms = earlier_squares + wide_last * wide_last
        moved = jnp.stack([partial] + [lax.ppermute(partial, ALL, perm_x[j]) for j in range(1, xs)])
        totals = moved[x % xs]
        for source in range(1, xs):
            totals = totals + moved[(x - source) % xs]
        total_shocks = shock_columns * xs
        shares = total_shocks * squared_terms / (totals[:, :, None] + 1e-06)
        return shares.reshape(local_rows, shock_columns)

    return on_device


def solution(mesh):
    rows = mesh.shape["rows"]
    xs = mesh.shape["shock"]
    zh = rows // (ZL * YS * CORE)
    mesh5 = Mesh(mesh.devices.reshape(zh, ZL, YS, CORE, xs), ALL)
    rows_axes = ("zh", "zl", "y", "c")
    placed = (
        P(rows_axes, None, None, None),
        P(),
        P(rows_axes, None),
        P(rows_axes),
        P("x"),
    )
    return jax.shard_map(
        make_body(zh, xs), mesh=mesh5, in_specs=placed, out_specs=P(rows_axes, "x"), check_vma=False
    )
```

```python
import numpy as np
import jax
import jax.numpy as jnp
from jax import lax
from jax.sharding import Mesh
from jax.sharding import PartitionSpec as P
from jax.experimental import pallas as pl
from jax.experimental.pallas import tpu as pltpu

HORIZONS = 7
CORE = 2
YS = 4
ZL = 2
ALL = ("zh", "zl", "y", "c", "x")
BOX = ("zl", "y", "c", "x")


def layout(zh, xs):
    zs = zh * ZL
    flat = lambda k, zl, y, c, x: (((k * ZL + zl) * YS + y) * CORE + c) * xs + x
    group_of = np.zeros((zh, ZL * YS * CORE * xs), np.int32)
    pos_of = np.zeros((zh, zs * YS * CORE), np.int32)
    zsrc = np.zeros((zh, ZL, YS, CORE, xs), np.int32)
    perm_in, perm_out = [], []
    for k in range(zh):
        for zl in range(ZL):
            for y in range(YS):
                for c in range(CORE):
                    for x in range(xs):
                        d = x if c == 0 else xs - 1 - x
                        z = (ZL * k - d) % zs if zl == 0 else (ZL * k + 1 + d) % zs
                        zsrc[k, zl, y, c, x] = z
                        g = (z * YS + y) * CORE + c
                        pos = ((zl * YS + y) * CORE + c) * xs + x
                        group_of[k, pos] = g
                        pos_of[k, g] = pos
                        src = flat(z // ZL, z % ZL, y, c, x)
                        me = flat(k, zl, y, c, x)
                        perm_in.append((src, me))
                        perm_out.append((me, flat(z // ZL, z % ZL, y, c, k)))
    perm_x = [
        [(flat(k, zl, y, c, x), flat(k, zl, y, c, (x + j) % xs)) for k in range(zh) for zl in range(ZL)
         for y in range(YS) for c in range(CORE) for x in range(xs)]
        for j in range(xs)
    ]
    return zsrc, group_of, pos_of, perm_in, perm_out, perm_x


def step_kernel(take_ref, send_ref, arrived_ref, coefs_ref, sq_ref, present_ref, sq_out_ref, out_hbm, lag_buf, sems):
    blk_dev, bs = coefs_ref.shape[0], coefs_ref.shape[1]
    lags = coefs_ref.shape[2] // bs
    for r in range(blk_dev):
        for l in range(lags):
            lag_buf[l * bs:(l + 1) * bs, :] = arrived_ref[take_ref[r * lags + l]]
        acc = jnp.dot(coefs_ref[r], lag_buf[...], preferred_element_type=jnp.float32)
        rounded = acc.astype(jnp.bfloat16)
        present_ref[r] = rounded
        wide = rounded.astype(jnp.float32)
        sq_out_ref[r] = sq_ref[r] + wide * wide
    if out_hbm is None:
        return
    copies = []
    for v in range(out_hbm.shape[0]):
        cp = pltpu.make_async_copy(present_ref.at[send_ref[v]], out_hbm.at[v], sems.at[v])
        cp.start()
        copies.append(cp)
    for cp in copies:
        cp.wait()


def last_kernel(take_ref, send_ref, arrived_ref, coefs_ref, sq_ref, present_ref, sq_out_ref, lag_buf, sems):
    step_kernel(take_ref, send_ref, arrived_ref, coefs_ref, sq_ref, present_ref, sq_out_ref, None, lag_buf, sems)


def step(take, send, arrived, coefs_wide, squares, last=False):
    blk_dev, bs, width = coefs_wide.shape
    cols = arrived.shape[2]
    n_out = send.shape[0]
    smem = pl.BlockSpec(memory_space=pltpu.SMEM)
    vmem = pl.BlockSpec(memory_space=pltpu.VMEM)
    hbm = pl.BlockSpec(memory_space=pl.ANY)
    shapes = (
        jax.ShapeDtypeStruct((blk_dev, bs, cols), jnp.bfloat16),
        jax.ShapeDtypeStruct((blk_dev, bs, cols), jnp.float32),
        jax.ShapeDtypeStruct((n_out, bs, cols), jnp.bfloat16),
    )
    return pl.pallas_call(
        last_kernel if last else step_kernel,
        out_shape=shapes[:2] if last else shapes,
        in_specs=[smem, smem, vmem, vmem, vmem],
        out_specs=(vmem, vmem) if last else (vmem, vmem, hbm),
        scratch_shapes=[
            pltpu.VMEM((width, cols), jnp.bfloat16),
            pltpu.SemaphoreType.DMA((n_out,)),
        ],
        input_output_aliases={4: 1},
    )(take, send, arrived, coefs_wide, squares)


def gather_rows(chosen, chosen_idio, owners):
    shocks, factors = chosen.shape
    per = shocks // owners
    packed = jnp.concatenate(
        [
            chosen.reshape(owners, per, factors),
            jnp.pad(chosen_idio.reshape(owners, 1, per), ((0, 0), (0, 0), (0, factors - per))),
        ],
        axis=1,
    )
    arrived = lax.all_to_all(packed, BOX, 0, 0, tiled=True)
    reduced = jnp.sum(arrived, axis=0, keepdims=True)
    spread = jnp.broadcast_to(reduced, packed.shape)
    full = lax.all_to_all(spread, BOX, 0, 0, tiled=True)
    return full[:, :per, :].reshape(shocks, factors), full[:, per, :per].reshape(shocks)


def make_body(zh, xs):
    zsrc_t, group_t, pos_t, perm_in, perm_out, perm_x = layout(zh, xs)

    def on_device(coefs, lag_pattern, loadings, idiosyncratic, shocked):
        loadings, idiosyncratic = lax.ppermute((loadings, idiosyncratic), ALL, perm_in)
        coefs = lax.ppermute(coefs, ALL, perm_in)
        blk_dev = coefs.shape[0]
        lags = coefs.shape[1]
        block_size = coefs.shape[2]
        k = lax.axis_index("zh")
        zl = lax.axis_index("zl")
        y = lax.axis_index("y")
        c = lax.axis_index("c")
        x = lax.axis_index("x")
        owners = ZL * YS * CORE * xs
        mine = (jnp.asarray(zsrc_t)[k, zl, y, c, x] * YS + y) * CORE + c
        group_of_pos = jnp.asarray(group_t)[k]
        pos_of_group = jnp.asarray(pos_t)[k]
        n_blocks = owners * blk_dev
        capacity = min(blk_dev, max(1, blk_dev * lags // owners))
        shifted = jnp.stack([shocked] + [lax.ppermute(shocked, ALL, perm_x[j]) for j in range(1, xs)])
        shock_columns = shocked.shape[0]
        shocked = shifted[(x - k) % xs]
        local_rows = blk_dev * block_size
        row_ids = mine * local_rows + jnp.arange(local_rows, dtype=jnp.int32)
        pick_table = (shocked[:, None] == row_ids[None, :]).astype(jnp.float32)
        chosen = jnp.dot(
            pick_table, loadings, precision=lax.Precision.HIGHEST, preferred_element_type=jnp.float32
        )
        chosen_idio = jnp.dot(
            pick_table,
            idiosyncratic,
            precision=lax.Precision.HIGHEST,
            preferred_element_type=jnp.float32,
        )
        chosen, chosen_idio = gather_rows(chosen, chosen_idio, owners)
        scale = jnp.sqrt(jnp.sum(chosen * chosen, axis=1) + chosen_idio)
        impact = jnp.dot(
            loadings, chosen.T, precision=lax.Precision.HIGHEST, preferred_element_type=jnp.float32
        )
        impact = impact + pick_table.T * idiosyncratic[:, None]
        impact = impact / scale[None, :]
        present_response = impact.astype(jnp.bfloat16).reshape(blk_dev, block_size, shock_columns)
        squared_terms = present_response.astype(jnp.float32) ** 2
        my_lags = lax.dynamic_slice_in_dim(lag_pattern, mine * blk_dev, blk_dev, 0)
        flat_lags = my_lags.reshape(-1)
        all_blocks_ids = jnp.arange(n_blocks, dtype=jnp.int32)
        read_need = jnp.any(flat_lags[:, None] == all_blocks_ids[None, :], axis=0).astype(jnp.int32)
        read_need = read_need.reshape(owners, blk_dev)[group_of_pos]
        read_before = jnp.cumsum(read_need, axis=1) - read_need
        owner_base = jnp.arange(owners, dtype=jnp.int32)[:, None] * capacity
        slot_of_pos = (owner_base + read_before).reshape(-1)
        block_at = pos_of_group[flat_lags // blk_dev] * blk_dev + flat_lags % blk_dev
        take_index = slot_of_pos[block_at]
        reader_slots = lag_pattern.reshape(owners, blk_dev * lags)[group_of_pos]
        own_ids = mine * blk_dev + jnp.arange(blk_dev, dtype=jnp.int32)
        send_need = jnp.any(reader_slots[:, :, None] == own_ids[None, None, :], axis=1).astype(
            jnp.int32
        )
        send_idx = jnp.argmax(send_need, axis=1).astype(jnp.int32)
        outgoing = jnp.take(present_response, send_idx, axis=0)
        coefs_wide = coefs.transpose(0, 2, 1, 3).reshape(blk_dev, block_size, lags * block_size)
        for step_no in range(HORIZONS - 1):
            arriving_response = lax.all_to_all(outgoing, BOX, split_axis=0, concat_axis=0, tiled=True)
            made = step(
                take_index, send_idx, arriving_response, coefs_wide, squared_terms,
                last=step_no == HORIZONS - 2,
            )
            present_response, squared_terms = made[:2]
            outgoing = made[-1]
        partial = jnp.sum(squared_terms, axis=2)
        squared_terms, partial = lax.ppermute((squared_terms, partial), ALL, perm_out)
        totals = lax.psum(partial, "x")
        total_shocks = shock_columns * xs
        shares = total_shocks * squared_terms / (totals[:, :, None] + 1e-06)
        return shares.reshape(local_rows, shock_columns)

    return on_device


def solution(mesh):
    rows = mesh.shape["rows"]
    xs = mesh.shape["shock"]
    zh = rows // (ZL * YS * CORE)
    mesh5 = Mesh(mesh.devices.reshape(zh, ZL, YS, CORE, xs), ALL)
    rows_axes = ("zh", "zl", "y", "c")
    placed = (
        P(rows_axes, None, None, None),
        P(),
        P(rows_axes, None),
        P(rows_axes),
        P("x"),
    )
    return jax.shard_map(
        make_body(zh, xs), mesh=mesh5, in_specs=placed, out_specs=P(rows_axes, "x"), check_vma=False
    )
```

```python
import numpy as np
import jax
import jax.numpy as jnp
from jax import lax
from jax.sharding import Mesh
from jax.sharding import PartitionSpec as P
from jax.experimental import pallas as pl
from jax.experimental.pallas import tpu as pltpu

HORIZONS = 7
CORE = 2
YS = 4
ZL = 2
ALL = ("zh", "zl", "y", "c", "x")
BOX = ("zl", "y", "c", "x")


def layout(zh, xs):
    zs = zh * ZL
    flat = lambda k, zl, y, c, x: (((k * ZL + zl) * YS + y) * CORE + c) * xs + x
    group_of = np.zeros((zh, ZL * YS * CORE * xs), np.int32)
    pos_of = np.zeros((zh, zs * YS * CORE), np.int32)
    zsrc = np.zeros((zh, ZL, YS, CORE, xs), np.int32)
    perm_in, perm_out = [], []
    for k in range(zh):
        for zl in range(ZL):
            for y in range(YS):
                for c in range(CORE):
                    for x in range(xs):
                        d = x if c == 0 else xs - 1 - x
                        z = (ZL * k - d) % zs if zl == 0 else (ZL * k + 1 + d) % zs
                        zsrc[k, zl, y, c, x] = z
                        g = (z * YS + y) * CORE + c
                        pos = ((zl * YS + y) * CORE + c) * xs + x
                        group_of[k, pos] = g
                        pos_of[k, g] = pos
                        src = flat(z // ZL, z % ZL, y, c, x)
                        me = flat(k, zl, y, c, x)
                        perm_in.append((src, me))
                        perm_out.append((me, flat(z // ZL, z % ZL, y, c, k)))
    perm_x = [
        [(flat(k, zl, y, c, x), flat(k, zl, y, c, (x + j) % xs)) for k in range(zh) for zl in range(ZL)
         for y in range(YS) for c in range(CORE) for x in range(xs)]
        for j in range(xs)
    ]
    return zsrc, group_of, pos_of, perm_in, perm_out, perm_x


def step_kernel(take_ref, send_ref, arrived_ref, coefs_ref, sq_ref, present_ref, sq_out_ref, out_hbm, lag_buf, sems):
    blk_dev, bs = coefs_ref.shape[0], coefs_ref.shape[1]
    lags = coefs_ref.shape[2] // bs
    for r in range(blk_dev):
        for l in range(lags):
            lag_buf[l * bs:(l + 1) * bs, :] = arrived_ref[take_ref[r * lags + l]]
        acc = jnp.dot(coefs_ref[r], lag_buf[...], preferred_element_type=jnp.float32)
        rounded = acc.astype(jnp.bfloat16)
        present_ref[r] = rounded
        wide = rounded.astype(jnp.float32)
        sq_out_ref[r] = sq_ref[r] + wide * wide
    if out_hbm is None:
        return
    copies = []
    for v in range(out_hbm.shape[0]):
        cp = pltpu.make_async_copy(present_ref.at[send_ref[v]], out_hbm.at[v], sems.at[v])
        cp.start()
        copies.append(cp)
    for cp in copies:
        cp.wait()


def last_kernel(take_ref, send_ref, arrived_ref, coefs_ref, sq_ref, present_ref, sq_out_ref, part_ref, lag_buf, sems):
    step_kernel(take_ref, send_ref, arrived_ref, coefs_ref, sq_ref, present_ref, sq_out_ref, None, lag_buf, sems)
    for r in range(part_ref.shape[0]):
        part_ref[r] = jnp.sum(sq_out_ref[r], axis=1)


def step(take, send, arrived, coefs_wide, squares, last=False):
    blk_dev, bs, width = coefs_wide.shape
    cols = arrived.shape[2]
    n_out = send.shape[0]
    smem = pl.BlockSpec(memory_space=pltpu.SMEM)
    vmem = pl.BlockSpec(memory_space=pltpu.VMEM)
    hbm = pl.BlockSpec(memory_space=pl.ANY)
    shapes = (
        jax.ShapeDtypeStruct((blk_dev, bs, cols), jnp.bfloat16),
        jax.ShapeDtypeStruct((blk_dev, bs, cols), jnp.float32),
        jax.ShapeDtypeStruct((n_out, bs, cols), jnp.bfloat16),
    )
    part = jax.ShapeDtypeStruct((blk_dev, bs), jnp.float32)
    return pl.pallas_call(
        last_kernel if last else step_kernel,
        out_shape=shapes[:2] + (part,) if last else shapes,
        in_specs=[smem, smem, vmem, vmem, vmem],
        out_specs=(vmem, vmem, vmem) if last else (vmem, vmem, hbm),
        scratch_shapes=[
            pltpu.VMEM((width, cols), jnp.bfloat16),
            pltpu.SemaphoreType.DMA((n_out,)),
        ],
        input_output_aliases={4: 1},
    )(take, send, arrived, coefs_wide, squares)


def gather_rows(chosen, chosen_idio, owners):
    shocks, factors = chosen.shape
    per = shocks // owners
    packed = jnp.concatenate(
        [
            chosen.reshape(owners, per, factors),
            jnp.pad(chosen_idio.reshape(owners, 1, per), ((0, 0), (0, 0), (0, factors - per))),
        ],
        axis=1,
    )
    arrived = lax.all_to_all(packed, BOX, 0, 0, tiled=True)
    reduced = jnp.sum(arrived, axis=0, keepdims=True)
    spread = jnp.broadcast_to(reduced, packed.shape)
    full = lax.all_to_all(spread, BOX, 0, 0, tiled=True)
    return full[:, :per, :].reshape(shocks, factors), full[:, per, :per].reshape(shocks)


def make_body(zh, xs):
    zsrc_t, group_t, pos_t, perm_in, perm_out, perm_x = layout(zh, xs)

    def on_device(coefs, lag_pattern, loadings, idiosyncratic, shocked):
        loadings, idiosyncratic = lax.ppermute((loadings, idiosyncratic), ALL, perm_in)
        coefs = lax.ppermute(coefs, ALL, perm_in)
        blk_dev = coefs.shape[0]
        lags = coefs.shape[1]
        block_size = coefs.shape[2]
        k = lax.axis_index("zh")
        zl = lax.axis_index("zl")
        y = lax.axis_index("y")
        c = lax.axis_index("c")
        x = lax.axis_index("x")
        owners = ZL * YS * CORE * xs
        mine = (jnp.asarray(zsrc_t)[k, zl, y, c, x] * YS + y) * CORE + c
        group_of_pos = jnp.asarray(group_t)[k]
        pos_of_group = jnp.asarray(pos_t)[k]
        n_blocks = owners * blk_dev
        capacity = min(blk_dev, max(1, blk_dev * lags // owners))
        shifted = jnp.stack([shocked] + [lax.ppermute(shocked, ALL, perm_x[j]) for j in range(1, xs)])
        shock_columns = shocked.shape[0]
        shocked = shifted[(x - k) % xs]
        local_rows = blk_dev * block_size
        row_ids = mine * local_rows + jnp.arange(local_rows, dtype=jnp.int32)
        pick_table = (shocked[:, None] == row_ids[None, :]).astype(jnp.float32)
        chosen = jnp.dot(
            pick_table, loadings, precision=lax.Precision.HIGHEST, preferred_element_type=jnp.float32
        )
        chosen_idio = jnp.dot(
            pick_table,
            idiosyncratic,
            precision=lax.Precision.HIGHEST,
            preferred_element_type=jnp.float32,
        )
        chosen, chosen_idio = gather_rows(chosen, chosen_idio, owners)
        scale = jnp.sqrt(jnp.sum(chosen * chosen, axis=1) + chosen_idio)
        impact = jnp.dot(
            loadings, chosen.T, precision=lax.Precision.HIGHEST, preferred_element_type=jnp.float32
        )
        impact = impact + pick_table.T * idiosyncratic[:, None]
        impact = impact / scale[None, :]
        present_response = impact.astype(jnp.bfloat16).reshape(blk_dev, block_size, shock_columns)
        squared_terms = present_response.astype(jnp.float32) ** 2
        my_lags = lax.dynamic_slice_in_dim(lag_pattern, mine * blk_dev, blk_dev, 0)
        flat_lags = my_lags.reshape(-1)
        all_blocks_ids = jnp.arange(n_blocks, dtype=jnp.int32)
        read_need = jnp.any(flat_lags[:, None] == all_blocks_ids[None, :], axis=0).astype(jnp.int32)
        read_need = read_need.reshape(owners, blk_dev)[group_of_pos]
        read_before = jnp.cumsum(read_need, axis=1) - read_need
        owner_base = jnp.arange(owners, dtype=jnp.int32)[:, None] * capacity
        slot_of_pos = (owner_base + read_before).reshape(-1)
        block_at = pos_of_group[flat_lags // blk_dev] * blk_dev + flat_lags % blk_dev
        take_index = slot_of_pos[block_at]
        reader_slots = lag_pattern.reshape(owners, blk_dev * lags)[group_of_pos]
        own_ids = mine * blk_dev + jnp.arange(blk_dev, dtype=jnp.int32)
        send_need = jnp.any(reader_slots[:, :, None] == own_ids[None, None, :], axis=1).astype(
            jnp.int32
        )
        send_idx = jnp.argmax(send_need, axis=1).astype(jnp.int32)
        outgoing = jnp.take(present_response, send_idx, axis=0)
        coefs_wide = coefs.transpose(0, 2, 1, 3).reshape(blk_dev, block_size, lags * block_size)
        for step_no in range(HORIZONS - 1):
            arriving_response = lax.all_to_all(outgoing, BOX, split_axis=0, concat_axis=0, tiled=True)
            made = step(
                take_index, send_idx, arriving_response, coefs_wide, squared_terms,
                last=step_no == HORIZONS - 2,
            )
            present_response, squared_terms = made[:2]
            outgoing = made[-1]
        partial = made[-1]
        squared_terms, partial = lax.ppermute((squared_terms, partial), ALL, perm_out)
        totals = lax.psum(partial, "x")
        total_shocks = shock_columns * xs
        shares = total_shocks * squared_terms / (totals[:, :, None] + 1e-06)
        return shares.reshape(local_rows, shock_columns)

    return on_device


def solution(mesh):
    rows = mesh.shape["rows"]
    xs = mesh.shape["shock"]
    zh = rows // (ZL * YS * CORE)
    mesh5 = Mesh(mesh.devices.reshape(zh, ZL, YS, CORE, xs), ALL)
    rows_axes = ("zh", "zl", "y", "c")
    placed = (
        P(rows_axes, None, None, None),
        P(),
        P(rows_axes, None),
        P(rows_axes),
        P("x"),
    )
    return jax.shard_map(
        make_body(zh, xs), mesh=mesh5, in_specs=placed, out_specs=P(rows_axes, "x"), check_vma=False
    )
```

```python
import numpy as np
import jax
import jax.numpy as jnp
from jax import lax
from jax.sharding import Mesh
from jax.sharding import PartitionSpec as P
from jax.experimental import pallas as pl
from jax.experimental.pallas import tpu as pltpu

HORIZONS = 7
CORE = 2
YS = 4
ZL = 2
ALL = ("zh", "zl", "y", "c", "x")
BOX = ("zl", "y", "c", "x")


def layout(zh, xs):
    zs = zh * ZL
    flat = lambda k, zl, y, c, x: (((k * ZL + zl) * YS + y) * CORE + c) * xs + x
    group_of = np.zeros((zh, ZL * YS * CORE * xs), np.int32)
    pos_of = np.zeros((zh, zs * YS * CORE), np.int32)
    zsrc = np.zeros((zh, ZL, YS, CORE, xs), np.int32)
    perm_in, perm_out = [], []
    for k in range(zh):
        for zl in range(ZL):
            for y in range(YS):
                for c in range(CORE):
                    for x in range(xs):
                        d = x if c == 0 else xs - 1 - x
                        z = (ZL * k - d) % zs if zl == 0 else (ZL * k + 1 + d) % zs
                        zsrc[k, zl, y, c, x] = z
                        g = (z * YS + y) * CORE + c
                        pos = ((zl * YS + y) * CORE + c) * xs + x
                        group_of[k, pos] = g
                        pos_of[k, g] = pos
                        src = flat(z // ZL, z % ZL, y, c, x)
                        me = flat(k, zl, y, c, x)
                        perm_in.append((src, me))
                        perm_out.append((me, flat(z // ZL, z % ZL, y, c, k)))
    perm_x = [
        [(flat(k, zl, y, c, x), flat(k, zl, y, c, (x + j) % xs)) for k in range(zh) for zl in range(ZL)
         for y in range(YS) for c in range(CORE) for x in range(xs)]
        for j in range(xs)
    ]
    return zsrc, group_of, pos_of, perm_in, perm_out, perm_x


def step_kernel(take_ref, send_ref, arrived_ref, coefs_ref, sq_ref, present_ref, sq_out_ref, out_hbm, lag_buf, sems):
    blk_dev, bs = coefs_ref.shape[0], coefs_ref.shape[1]
    lags = coefs_ref.shape[2] // bs
    for r in range(blk_dev):
        for l in range(lags):
            lag_buf[l * bs:(l + 1) * bs, :] = arrived_ref[take_ref[r * lags + l]]
        acc = jnp.dot(coefs_ref[r], lag_buf[...], preferred_element_type=jnp.float32)
        rounded = acc.astype(jnp.bfloat16)
        present_ref[r] = rounded
        wide = rounded.astype(jnp.float32)
        sq_out_ref[r] = sq_ref[r] + wide * wide
    if out_hbm is None:
        return
    copies = []
    for v in range(out_hbm.shape[0]):
        cp = pltpu.make_async_copy(present_ref.at[send_ref[v]], out_hbm.at[v], sems.at[v])
        cp.start()
        copies.append(cp)
    for cp in copies:
        cp.wait()


def last_kernel(take_ref, send_ref, arrived_ref, coefs_ref, sq_ref, present_ref, sq_out_ref, lag_buf, sems):
    step_kernel(take_ref, send_ref, arrived_ref, coefs_ref, sq_ref, present_ref, sq_out_ref, None, lag_buf, sems)


def step(take, send, arrived, coefs_wide, squares, last=False):
    blk_dev, bs, width = coefs_wide.shape
    cols = arrived.shape[2]
    n_out = send.shape[0]
    smem = pl.BlockSpec(memory_space=pltpu.SMEM)
    vmem = pl.BlockSpec(memory_space=pltpu.VMEM)
    hbm = pl.BlockSpec(memory_space=pl.ANY)
    shapes = (
        jax.ShapeDtypeStruct((blk_dev, bs, cols), jnp.bfloat16),
        jax.ShapeDtypeStruct((blk_dev, bs, cols), jnp.float32),
        jax.ShapeDtypeStruct((n_out, bs, cols), jnp.bfloat16),
    )
    return pl.pallas_call(
        last_kernel if last else step_kernel,
        out_shape=shapes[:2] if last else shapes,
        in_specs=[smem, smem, vmem, vmem, vmem],
        out_specs=(vmem, vmem) if last else (vmem, vmem, hbm),
        scratch_shapes=[
            pltpu.VMEM((width, cols), jnp.bfloat16),
            pltpu.SemaphoreType.DMA((n_out,)),
        ],
        input_output_aliases={4: 1},
    )(take, send, arrived, coefs_wide, squares)


def gather_rows(chosen, chosen_idio, owners):
    shocks, factors = chosen.shape
    per = shocks // owners
    packed = jnp.concatenate(
        [
            chosen.reshape(owners, per, factors),
            jnp.pad(chosen_idio.reshape(owners, 1, per), ((0, 0), (0, 0), (0, factors - per))),
        ],
        axis=1,
    )
    arrived = lax.all_to_all(packed, BOX, 0, 0, tiled=True)
    reduced = jnp.sum(arrived, axis=0, keepdims=True)
    spread = jnp.broadcast_to(reduced, packed.shape)
    full = lax.all_to_all(spread, BOX, 0, 0, tiled=True)
    return full[:, :per, :].reshape(shocks, factors), full[:, per, :per].reshape(shocks)


def make_body(zh, xs):
    zsrc_t, group_t, pos_t, perm_in, perm_out, perm_x = layout(zh, xs)

    moves_in = [(a, b) for a, b in perm_in if a != b]
    moves_out = [(a, b) for a, b in perm_out if a != b]
    stays_in = np.array([a == b for a, b in sorted(perm_in, key=lambda p: p[1])])
    stays_out = np.array([a == b for a, b in sorted(perm_out, key=lambda p: p[1])])

    def move(value, moves, stays, me):
        moved = lax.ppermute(value, ALL, moves)
        return jax.tree.map(lambda own, got: jnp.where(jnp.asarray(stays)[me], own, got), value, moved)

    def on_device(coefs, lag_pattern, loadings, idiosyncratic, shocked):
        me = lax.axis_index(ALL)
        loadings, idiosyncratic = move((loadings, idiosyncratic), moves_in, stays_in, me)
        coefs = move(coefs, moves_in, stays_in, me)
        blk_dev = coefs.shape[0]
        lags = coefs.shape[1]
        block_size = coefs.shape[2]
        k = lax.axis_index("zh")
        zl = lax.axis_index("zl")
        y = lax.axis_index("y")
        c = lax.axis_index("c")
        x = lax.axis_index("x")
        owners = ZL * YS * CORE * xs
        mine = (jnp.asarray(zsrc_t)[k, zl, y, c, x] * YS + y) * CORE + c
        group_of_pos = jnp.asarray(group_t)[k]
        pos_of_group = jnp.asarray(pos_t)[k]
        n_blocks = owners * blk_dev
        capacity = min(blk_dev, max(1, blk_dev * lags // owners))
        shifted = jnp.stack([shocked] + [lax.ppermute(shocked, ALL, perm_x[j]) for j in range(1, xs)])
        shock_columns = shocked.shape[0]
        shocked = shifted[(x - k) % xs]
        local_rows = blk_dev * block_size
        row_ids = mine * local_rows + jnp.arange(local_rows, dtype=jnp.int32)
        pick_table = (shocked[:, None] == row_ids[None, :]).astype(jnp.float32)
        chosen = jnp.dot(
            pick_table, loadings, precision=lax.Precision.HIGHEST, preferred_element_type=jnp.float32
        )
        chosen_idio = jnp.dot(
            pick_table,
            idiosyncratic,
            precision=lax.Precision.HIGHEST,
            preferred_element_type=jnp.float32,
        )
        chosen, chosen_idio = gather_rows(chosen, chosen_idio, owners)
        scale = jnp.sqrt(jnp.sum(chosen * chosen, axis=1) + chosen_idio)
        impact = jnp.dot(
            loadings, chosen.T, precision=lax.Precision.HIGHEST, preferred_element_type=jnp.float32
        )
        impact = impact + pick_table.T * idiosyncratic[:, None]
        impact = impact / scale[None, :]
        present_response = impact.astype(jnp.bfloat16).reshape(blk_dev, block_size, shock_columns)
        squared_terms = present_response.astype(jnp.float32) ** 2
        my_lags = lax.dynamic_slice_in_dim(lag_pattern, mine * blk_dev, blk_dev, 0)
        flat_lags = my_lags.reshape(-1)
        all_blocks_ids = jnp.arange(n_blocks, dtype=jnp.int32)
        read_need = jnp.any(flat_lags[:, None] == all_blocks_ids[None, :], axis=0).astype(jnp.int32)
        read_need = read_need.reshape(owners, blk_dev)[group_of_pos]
        read_before = jnp.cumsum(read_need, axis=1) - read_need
        owner_base = jnp.arange(owners, dtype=jnp.int32)[:, None] * capacity
        slot_of_pos = (owner_base + read_before).reshape(-1)
        block_at = pos_of_group[flat_lags // blk_dev] * blk_dev + flat_lags % blk_dev
        take_index = slot_of_pos[block_at]
        reader_slots = lag_pattern.reshape(owners, blk_dev * lags)[group_of_pos]
        own_ids = mine * blk_dev + jnp.arange(blk_dev, dtype=jnp.int32)
        send_need = jnp.any(reader_slots[:, :, None] == own_ids[None, None, :], axis=1).astype(
            jnp.int32
        )
        send_idx = jnp.argmax(send_need, axis=1).astype(jnp.int32)
        outgoing = jnp.take(present_response, send_idx, axis=0)
        coefs_wide = coefs.transpose(0, 2, 1, 3).reshape(blk_dev, block_size, lags * block_size)
        for step_no in range(HORIZONS - 1):
            arriving_response = lax.all_to_all(outgoing, BOX, split_axis=0, concat_axis=0, tiled=True)
            made = step(
                take_index, send_idx, arriving_response, coefs_wide, squared_terms,
                last=step_no == HORIZONS - 2,
            )
            present_response, squared_terms = made[:2]
            outgoing = made[-1]
        partial = jnp.sum(squared_terms, axis=2)
        squared_terms, partial = move((squared_terms, partial), moves_out, stays_out, me)
        totals = lax.psum(partial, "x")
        total_shocks = shock_columns * xs
        shares = total_shocks * squared_terms / (totals[:, :, None] + 1e-06)
        return shares.reshape(local_rows, shock_columns)

    return on_device


def solution(mesh):
    rows = mesh.shape["rows"]
    xs = mesh.shape["shock"]
    zh = rows // (ZL * YS * CORE)
    mesh5 = Mesh(mesh.devices.reshape(zh, ZL, YS, CORE, xs), ALL)
    rows_axes = ("zh", "zl", "y", "c")
    placed = (
        P(rows_axes, None, None, None),
        P(),
        P(rows_axes, None),
        P(rows_axes),
        P("x"),
    )
    return jax.shard_map(
        make_body(zh, xs), mesh=mesh5, in_specs=placed, out_specs=P(rows_axes, "x"), check_vma=False
    )
```

```python
import numpy as np
import jax
import jax.numpy as jnp
from jax import lax
from jax.sharding import Mesh
from jax.sharding import PartitionSpec as P
from jax.experimental import pallas as pl
from jax.experimental.pallas import tpu as pltpu

HORIZONS = 7
CORE = 2
YS = 4
ZL = 2
ALL = ("zh", "zl", "y", "c", "x")
BOX = ("zl", "y", "c", "x")


def layout(zh, xs):
    zs = zh * ZL
    flat = lambda k, zl, y, c, x: (((k * ZL + zl) * YS + y) * CORE + c) * xs + x
    group_of = np.zeros((zh, ZL * YS * CORE * xs), np.int32)
    pos_of = np.zeros((zh, zs * YS * CORE), np.int32)
    zsrc = np.zeros((zh, ZL, YS, CORE, xs), np.int32)
    perm_in, perm_out = [], []
    for k in range(zh):
        for zl in range(ZL):
            for y in range(YS):
                for c in range(CORE):
                    for x in range(xs):
                        d = x if c == 0 else xs - 1 - x
                        z = (ZL * k - d) % zs if zl == 0 else (ZL * k + 1 + d) % zs
                        zsrc[k, zl, y, c, x] = z
                        g = (z * YS + y) * CORE + c
                        pos = ((zl * YS + y) * CORE + c) * xs + x
                        group_of[k, pos] = g
                        pos_of[k, g] = pos
                        src = flat(z // ZL, z % ZL, y, c, x)
                        me = flat(k, zl, y, c, x)
                        perm_in.append((src, me))
                        perm_out.append((me, flat(z // ZL, z % ZL, y, c, k)))
    perm_x = [
        [(flat(k, zl, y, c, x), flat(k, zl, y, c, (x + j) % xs)) for k in range(zh) for zl in range(ZL)
         for y in range(YS) for c in range(CORE) for x in range(xs)]
        for j in range(xs)
    ]
    return zsrc, group_of, pos_of, perm_in, perm_out, perm_x


def step_kernel(take_ref, send_ref, arrived_ref, coefs_ref, sq_ref, present_ref, sq_out_ref, out_hbm, lag_buf, sems):
    blk_dev, bs = coefs_ref.shape[0], coefs_ref.shape[1]
    lags = coefs_ref.shape[2] // bs
    for r in range(blk_dev):
        for l in range(lags):
            lag_buf[l * bs:(l + 1) * bs, :] = arrived_ref[take_ref[r * lags + l]]
        acc = jnp.dot(coefs_ref[r], lag_buf[...], preferred_element_type=jnp.float32)
        rounded = acc.astype(jnp.bfloat16)
        present_ref[r] = rounded
        wide = rounded.astype(jnp.float32)
        sq_out_ref[r] = sq_ref[r] + wide * wide
    if out_hbm is None:
        return
    copies = []
    for v in range(out_hbm.shape[0]):
        cp = pltpu.make_async_copy(present_ref.at[send_ref[v]], out_hbm.at[v], sems.at[v])
        cp.start()
        copies.append(cp)
    for cp in copies:
        cp.wait()


def last_kernel(take_ref, send_ref, arrived_ref, coefs_ref, sq_ref, present_ref, sq_out_ref, lag_buf, sems):
    step_kernel(take_ref, send_ref, arrived_ref, coefs_ref, sq_ref, present_ref, sq_out_ref, None, lag_buf, sems)


def step(take, send, arrived, coefs_wide, squares, last=False):
    blk_dev, bs, width = coefs_wide.shape
    cols = arrived.shape[2]
    n_out = send.shape[0]
    smem = pl.BlockSpec(memory_space=pltpu.SMEM)
    vmem = pl.BlockSpec(memory_space=pltpu.VMEM)
    hbm = pl.BlockSpec(memory_space=pl.ANY)
    shapes = (
        jax.ShapeDtypeStruct((blk_dev, bs, cols), jnp.bfloat16),
        jax.ShapeDtypeStruct((blk_dev, bs, cols), jnp.float32),
        jax.ShapeDtypeStruct((n_out, bs, cols), jnp.bfloat16),
    )
    return pl.pallas_call(
        last_kernel if last else step_kernel,
        out_shape=shapes[:2] if last else shapes,
        in_specs=[smem, smem, vmem, vmem, vmem],
        out_specs=(vmem, vmem) if last else (vmem, vmem, hbm),
        scratch_shapes=[
            pltpu.VMEM((width, cols), jnp.bfloat16),
            pltpu.SemaphoreType.DMA((n_out,)),
        ],
        input_output_aliases={4: 1},
    )(take, send, arrived, coefs_wide, squares)


def gather_rows(chosen, chosen_idio, owners):
    shocks, factors = chosen.shape
    per = shocks // owners
    packed = jnp.concatenate(
        [
            chosen.reshape(owners, per, factors),
            jnp.pad(chosen_idio.reshape(owners, 1, per), ((0, 0), (0, 0), (0, factors - per))),
        ],
        axis=1,
    )
    arrived = lax.all_to_all(packed, BOX, 0, 0, tiled=True)
    reduced = jnp.sum(arrived, axis=0, keepdims=True)
    spread = jnp.broadcast_to(reduced, packed.shape)
    full = lax.all_to_all(spread, BOX, 0, 0, tiled=True)
    return full[:, :per, :].reshape(shocks, factors), full[:, per, :per].reshape(shocks)


def make_body(zh, xs):
    zsrc_t, group_t, pos_t, perm_in, perm_out, perm_x = layout(zh, xs)

    def on_device(coefs, lag_pattern, loadings, idiosyncratic, shocked):
        loadings, idiosyncratic = lax.ppermute((loadings, idiosyncratic), ALL, perm_in)
        blk_dev = coefs.shape[0]
        lags = coefs.shape[1]
        block_size = coefs.shape[2]
        k = lax.axis_index("zh")
        zl = lax.axis_index("zl")
        y = lax.axis_index("y")
        c = lax.axis_index("c")
        x = lax.axis_index("x")
        owners = ZL * YS * CORE * xs
        mine = (jnp.asarray(zsrc_t)[k, zl, y, c, x] * YS + y) * CORE + c
        group_of_pos = jnp.asarray(group_t)[k]
        pos_of_group = jnp.asarray(pos_t)[k]
        n_blocks = owners * blk_dev
        capacity = min(blk_dev, max(1, blk_dev * lags // owners))
        shifted = jnp.stack([shocked] + [lax.ppermute(shocked, ALL, perm_x[j]) for j in range(1, xs)])
        shock_columns = shocked.shape[0]
        shocked = shifted[(x - k) % xs]
        local_rows = blk_dev * block_size
        row_ids = mine * local_rows + jnp.arange(local_rows, dtype=jnp.int32)
        pick_table = (shocked[:, None] == row_ids[None, :]).astype(jnp.float32)
        chosen = jnp.dot(
            pick_table, loadings, precision=lax.Precision.HIGHEST, preferred_element_type=jnp.float32
        )
        chosen_idio = jnp.dot(
            pick_table,
            idiosyncratic,
            precision=lax.Precision.HIGHEST,
            preferred_element_type=jnp.float32,
        )
        chosen, chosen_idio = gather_rows(chosen, chosen_idio, owners)
        scale = jnp.sqrt(jnp.sum(chosen * chosen, axis=1) + chosen_idio)
        impact = jnp.dot(
            loadings, chosen.T, precision=lax.Precision.HIGHEST, preferred_element_type=jnp.float32
        )
        impact = impact + pick_table.T * idiosyncratic[:, None]
        impact = impact / scale[None, :]
        present_response = impact.astype(jnp.bfloat16).reshape(blk_dev, block_size, shock_columns)
        squared_terms = present_response.astype(jnp.float32) ** 2
        my_lags = lax.dynamic_slice_in_dim(lag_pattern, mine * blk_dev, blk_dev, 0)
        flat_lags = my_lags.reshape(-1)
        all_blocks_ids = jnp.arange(n_blocks, dtype=jnp.int32)
        read_need = jnp.any(flat_lags[:, None] == all_blocks_ids[None, :], axis=0).astype(jnp.int32)
        read_need = read_need.reshape(owners, blk_dev)[group_of_pos]
        read_before = jnp.cumsum(read_need, axis=1) - read_need
        owner_base = jnp.arange(owners, dtype=jnp.int32)[:, None] * capacity
        slot_of_pos = (owner_base + read_before).reshape(-1)
        block_at = pos_of_group[flat_lags // blk_dev] * blk_dev + flat_lags % blk_dev
        take_index = slot_of_pos[block_at]
        reader_slots = lag_pattern.reshape(owners, blk_dev * lags)[group_of_pos]
        own_ids = mine * blk_dev + jnp.arange(blk_dev, dtype=jnp.int32)
        send_need = jnp.any(reader_slots[:, :, None] == own_ids[None, None, :], axis=1).astype(
            jnp.int32
        )
        send_idx = jnp.argmax(send_need, axis=1).astype(jnp.int32)
        outgoing = jnp.take(present_response, send_idx, axis=0)
        coefs_wide = coefs.transpose(0, 2, 1, 3).reshape(blk_dev, block_size, lags * block_size)
        for step_no in range(HORIZONS - 1):
            arriving_response = lax.all_to_all(outgoing, BOX, split_axis=0, concat_axis=0, tiled=True)
            if step_no == 0:
                arriving_response, coefs_wide = lax.optimization_barrier((arriving_response, coefs_wide))
                coefs_wide = lax.ppermute(coefs_wide, ALL, perm_in)
            made = step(
                take_index, send_idx, arriving_response, coefs_wide, squared_terms,
                last=step_no == HORIZONS - 2,
            )
            present_response, squared_terms = made[:2]
            outgoing = made[-1]
        partial = jnp.sum(squared_terms, axis=2)
        squared_terms, partial = lax.ppermute((squared_terms, partial), ALL, perm_out)
        totals = lax.psum(partial, "x")
        total_shocks = shock_columns * xs
        shares = total_shocks * squared_terms / (totals[:, :, None] + 1e-06)
        return shares.reshape(local_rows, shock_columns)

    return on_device


def solution(mesh):
    rows = mesh.shape["rows"]
    xs = mesh.shape["shock"]
    zh = rows // (ZL * YS * CORE)
    mesh5 = Mesh(mesh.devices.reshape(zh, ZL, YS, CORE, xs), ALL)
    rows_axes = ("zh", "zl", "y", "c")
    placed = (
        P(rows_axes, None, None, None),
        P(),
        P(rows_axes, None),
        P(rows_axes),
        P("x"),
    )
    return jax.shard_map(
        make_body(zh, xs), mesh=mesh5, in_specs=placed, out_specs=P(rows_axes, "x"), check_vma=False
    )
```

```python
import numpy as np
import jax
import jax.numpy as jnp
from jax import lax
from jax.sharding import Mesh
from jax.sharding import PartitionSpec as P
from jax.experimental import pallas as pl
from jax.experimental.pallas import tpu as pltpu

HORIZONS = 7
CORE = 2
YS = 4
ZL = 2
ALL = ("zh", "zl", "y", "c", "x")
BOX = ("zl", "y", "c", "x")


def layout(zh, xs):
    zs = zh * ZL
    flat = lambda k, zl, y, c, x: (((k * ZL + zl) * YS + y) * CORE + c) * xs + x
    group_of = np.zeros((zh, ZL * YS * CORE * xs), np.int32)
    pos_of = np.zeros((zh, zs * YS * CORE), np.int32)
    zsrc = np.zeros((zh, ZL, YS, CORE, xs), np.int32)
    perm_in, perm_out = [], []
    for k in range(zh):
        for zl in range(ZL):
            for y in range(YS):
                for c in range(CORE):
                    for x in range(xs):
                        d = x if c == 0 else xs - 1 - x
                        z = (ZL * k - d) % zs if zl == 0 else (ZL * k + 1 + d) % zs
                        zsrc[k, zl, y, c, x] = z
                        g = (z * YS + y) * CORE + c
                        pos = ((zl * YS + y) * CORE + c) * xs + x
                        group_of[k, pos] = g
                        pos_of[k, g] = pos
                        src = flat(z // ZL, z % ZL, y, c, x)
                        me = flat(k, zl, y, c, x)
                        perm_in.append((src, me))
                        perm_out.append((me, flat(z // ZL, z % ZL, y, c, k)))
    perm_x = [
        [(flat(k, zl, y, c, x), flat(k, zl, y, c, (x + j) % xs)) for k in range(zh) for zl in range(ZL)
         for y in range(YS) for c in range(CORE) for x in range(xs)]
        for j in range(xs)
    ]
    return zsrc, group_of, pos_of, perm_in, perm_out, perm_x


def step_kernel(take_ref, send_ref, arrived_ref, coefs_ref, sq_ref, present_ref, sq_out_ref, out_hbm, lag_buf, sems):
    blk_dev, bs = coefs_ref.shape[0], coefs_ref.shape[1]
    lags = coefs_ref.shape[2] // bs
    for r in range(blk_dev):
        for l in range(lags):
            lag_buf[l * bs:(l + 1) * bs, :] = arrived_ref[take_ref[r * lags + l]]
        acc = jnp.dot(coefs_ref[r], lag_buf[...], preferred_element_type=jnp.float32)
        rounded = acc.astype(jnp.bfloat16)
        present_ref[r] = rounded
        wide = rounded.astype(jnp.float32)
        sq_out_ref[r] = sq_ref[r] + wide * wide
    if out_hbm is None:
        return
    copies = []
    for v in range(out_hbm.shape[0]):
        cp = pltpu.make_async_copy(present_ref.at[send_ref[v]], out_hbm.at[v], sems.at[v])
        cp.start()
        copies.append(cp)
    for cp in copies:
        cp.wait()


def last_kernel(take_ref, send_ref, arrived_ref, coefs_ref, sq_ref, present_ref, sq_out_ref, lag_buf, sems):
    step_kernel(take_ref, send_ref, arrived_ref, coefs_ref, sq_ref, present_ref, sq_out_ref, None, lag_buf, sems)


def step(take, send, arrived, coefs_wide, squares, last=False):
    blk_dev, bs, width = coefs_wide.shape
    cols = arrived.shape[2]
    n_out = send.shape[0]
    smem = pl.BlockSpec(memory_space=pltpu.SMEM)
    vmem = pl.BlockSpec(memory_space=pltpu.VMEM)
    hbm = pl.BlockSpec(memory_space=pl.ANY)
    shapes = (
        jax.ShapeDtypeStruct((blk_dev, bs, cols), jnp.bfloat16),
        jax.ShapeDtypeStruct((blk_dev, bs, cols), jnp.float32),
        jax.ShapeDtypeStruct((n_out, bs, cols), jnp.bfloat16),
    )
    return pl.pallas_call(
        last_kernel if last else step_kernel,
        out_shape=shapes[:2] if last else shapes,
        in_specs=[smem, smem, vmem, vmem, vmem],
        out_specs=(vmem, vmem) if last else (vmem, vmem, hbm),
        scratch_shapes=[
            pltpu.VMEM((width, cols), jnp.bfloat16),
            pltpu.SemaphoreType.DMA((n_out,)),
        ],
        input_output_aliases={4: 1},
    )(take, send, arrived, coefs_wide, squares)


def gather_rows(chosen, chosen_idio, owners):
    shocks, factors = chosen.shape
    per = shocks // owners
    packed = jnp.concatenate(
        [
            chosen.reshape(owners, per, factors),
            jnp.pad(chosen_idio.reshape(owners, 1, per), ((0, 0), (0, 0), (0, factors - per))),
        ],
        axis=1,
    )
    arrived = lax.all_to_all(packed, BOX, 0, 0, tiled=True)
    reduced = jnp.sum(arrived, axis=0, keepdims=True)
    spread = jnp.broadcast_to(reduced, packed.shape)
    full = lax.all_to_all(spread, BOX, 0, 0, tiled=True)
    return full[:, :per, :].reshape(shocks, factors), full[:, per, :per].reshape(shocks)


def make_body(zh, xs):
    zsrc_t, group_t, pos_t, perm_in, perm_out, perm_x = layout(zh, xs)

    def on_device(coefs, lag_pattern, loadings, idiosyncratic, shocked):
        loadings, idiosyncratic = lax.ppermute((loadings, idiosyncratic), ALL, perm_in)
        coefs = lax.ppermute(coefs, ALL, perm_in)
        loadings, coefs = lax.optimization_barrier((loadings, coefs))
        blk_dev = coefs.shape[0]
        lags = coefs.shape[1]
        block_size = coefs.shape[2]
        k = lax.axis_index("zh")
        zl = lax.axis_index("zl")
        y = lax.axis_index("y")
        c = lax.axis_index("c")
        x = lax.axis_index("x")
        owners = ZL * YS * CORE * xs
        mine = (jnp.asarray(zsrc_t)[k, zl, y, c, x] * YS + y) * CORE + c
        group_of_pos = jnp.asarray(group_t)[k]
        pos_of_group = jnp.asarray(pos_t)[k]
        n_blocks = owners * blk_dev
        capacity = min(blk_dev, max(1, blk_dev * lags // owners))
        shifted = jnp.stack([shocked] + [lax.ppermute(shocked, ALL, perm_x[j]) for j in range(1, xs)])
        shock_columns = shocked.shape[0]
        shocked = shifted[(x - k) % xs]
        local_rows = blk_dev * block_size
        row_ids = mine * local_rows + jnp.arange(local_rows, dtype=jnp.int32)
        pick_table = (shocked[:, None] == row_ids[None, :]).astype(jnp.float32)
        chosen = jnp.dot(
            pick_table, loadings, precision=lax.Precision.HIGHEST, preferred_element_type=jnp.float32
        )
        chosen_idio = jnp.dot(
            pick_table,
            idiosyncratic,
            precision=lax.Precision.HIGHEST,
            preferred_element_type=jnp.float32,
        )
        chosen, chosen_idio = gather_rows(chosen, chosen_idio, owners)
        scale = jnp.sqrt(jnp.sum(chosen * chosen, axis=1) + chosen_idio)
        impact = jnp.dot(
            loadings, chosen.T, precision=lax.Precision.HIGHEST, preferred_element_type=jnp.float32
        )
        impact = impact + pick_table.T * idiosyncratic[:, None]
        impact = impact / scale[None, :]
        present_response = impact.astype(jnp.bfloat16).reshape(blk_dev, block_size, shock_columns)
        squared_terms = present_response.astype(jnp.float32) ** 2
        my_lags = lax.dynamic_slice_in_dim(lag_pattern, mine * blk_dev, blk_dev, 0)
        flat_lags = my_lags.reshape(-1)
        all_blocks_ids = jnp.arange(n_blocks, dtype=jnp.int32)
        read_need = jnp.any(flat_lags[:, None] == all_blocks_ids[None, :], axis=0).astype(jnp.int32)
        read_need = read_need.reshape(owners, blk_dev)[group_of_pos]
        read_before = jnp.cumsum(read_need, axis=1) - read_need
        owner_base = jnp.arange(owners, dtype=jnp.int32)[:, None] * capacity
        slot_of_pos = (owner_base + read_before).reshape(-1)
        block_at = pos_of_group[flat_lags // blk_dev] * blk_dev + flat_lags % blk_dev
        take_index = slot_of_pos[block_at]
        reader_slots = lag_pattern.reshape(owners, blk_dev * lags)[group_of_pos]
        own_ids = mine * blk_dev + jnp.arange(blk_dev, dtype=jnp.int32)
        send_need = jnp.any(reader_slots[:, :, None] == own_ids[None, None, :], axis=1).astype(
            jnp.int32
        )
        send_idx = jnp.argmax(send_need, axis=1).astype(jnp.int32)
        outgoing = jnp.take(present_response, send_idx, axis=0)
        coefs_wide = coefs.transpose(0, 2, 1, 3).reshape(blk_dev, block_size, lags * block_size)
        for step_no in range(HORIZONS - 1):
            arriving_response = lax.all_to_all(outgoing, BOX, split_axis=0, concat_axis=0, tiled=True)
            made = step(
                take_index, send_idx, arriving_response, coefs_wide, squared_terms,
                last=step_no == HORIZONS - 2,
            )
            present_response, squared_terms = made[:2]
            outgoing = made[-1]
        partial = jnp.sum(squared_terms, axis=2)
        squared_terms, partial = lax.ppermute((squared_terms, partial), ALL, perm_out)
        totals = lax.psum(partial, "x")
        total_shocks = shock_columns * xs
        shares = total_shocks * squared_terms / (totals[:, :, None] + 1e-06)
        return shares.reshape(local_rows, shock_columns)

    return on_device


def solution(mesh):
    rows = mesh.shape["rows"]
    xs = mesh.shape["shock"]
    zh = rows // (ZL * YS * CORE)
    mesh5 = Mesh(mesh.devices.reshape(zh, ZL, YS, CORE, xs), ALL)
    rows_axes = ("zh", "zl", "y", "c")
    placed = (
        P(rows_axes, None, None, None),
        P(),
        P(rows_axes, None),
        P(rows_axes),
        P("x"),
    )
    return jax.shard_map(
        make_body(zh, xs), mesh=mesh5, in_specs=placed, out_specs=P(rows_axes, "x"), check_vma=False
    )
```

```python
import numpy as np
import jax
import jax.numpy as jnp
from jax import lax
from jax.sharding import Mesh
from jax.sharding import PartitionSpec as P
from jax.experimental import pallas as pl
from jax.experimental.pallas import tpu as pltpu

HORIZONS = 7
CORE = 2
YS = 4
ZL = 2
ALL = ("zh", "zl", "y", "c", "x")
BOX = ("zl", "y", "c", "x")


def layout(zh, xs):
    zs = zh * ZL
    flat = lambda k, zl, y, c, x: (((k * ZL + zl) * YS + y) * CORE + c) * xs + x
    group_of = np.zeros((zh, ZL * YS * CORE * xs), np.int32)
    pos_of = np.zeros((zh, zs * YS * CORE), np.int32)
    zsrc = np.zeros((zh, ZL, YS, CORE, xs), np.int32)
    perm_in, perm_out = [], []
    for k in range(zh):
        for zl in range(ZL):
            for y in range(YS):
                for c in range(CORE):
                    for x in range(xs):
                        d = x if c == 0 else xs - 1 - x
                        z = (ZL * k - d) % zs if zl == 0 else (ZL * k + 1 + d) % zs
                        zsrc[k, zl, y, c, x] = z
                        g = (z * YS + y) * CORE + c
                        pos = ((zl * YS + y) * CORE + c) * xs + x
                        group_of[k, pos] = g
                        pos_of[k, g] = pos
                        src = flat(z // ZL, z % ZL, y, c, x)
                        me = flat(k, zl, y, c, x)
                        perm_in.append((src, me))
                        perm_out.append((me, flat(z // ZL, z % ZL, y, c, k)))
    perm_x = [
        [(flat(k, zl, y, c, x), flat(k, zl, y, c, (x + j) % xs)) for k in range(zh) for zl in range(ZL)
         for y in range(YS) for c in range(CORE) for x in range(xs)]
        for j in range(xs)
    ]
    return zsrc, group_of, pos_of, perm_in, perm_out, perm_x


def step_kernel(take_ref, send_ref, arrived_ref, coefs_ref, sq_ref, present_ref, sq_out_ref, out_hbm, lag_buf, sems):
    blk_dev, bs = coefs_ref.shape[0], coefs_ref.shape[1]
    lags = coefs_ref.shape[2] // bs
    for r in range(blk_dev):
        for l in range(lags):
            lag_buf[l * bs:(l + 1) * bs, :] = arrived_ref[take_ref[r * lags + l]]
        acc = jnp.dot(coefs_ref[r], lag_buf[...], preferred_element_type=jnp.float32)
        rounded = acc.astype(jnp.bfloat16)
        present_ref[r] = rounded
        wide = rounded.astype(jnp.float32)
        sq_out_ref[r] = sq_ref[r] + wide * wide
    if out_hbm is None:
        return
    copies = []
    for v in range(out_hbm.shape[0]):
        cp = pltpu.make_async_copy(present_ref.at[send_ref[v]], out_hbm.at[v], sems.at[v])
        cp.start()
        copies.append(cp)
    for cp in copies:
        cp.wait()


def last_kernel(take_ref, send_ref, arrived_ref, coefs_ref, sq_ref, present_ref, sq_out_ref, lag_buf, sems):
    step_kernel(take_ref, send_ref, arrived_ref, coefs_ref, sq_ref, present_ref, sq_out_ref, None, lag_buf, sems)


def step(take, send, arrived, coefs_wide, squares, last=False):
    blk_dev, bs, width = coefs_wide.shape
    cols = arrived.shape[2]
    n_out = send.shape[0]
    smem = pl.BlockSpec(memory_space=pltpu.SMEM)
    vmem = pl.BlockSpec(memory_space=pltpu.VMEM)
    hbm = pl.BlockSpec(memory_space=pl.ANY)
    shapes = (
        jax.ShapeDtypeStruct((blk_dev, bs, cols), jnp.bfloat16),
        jax.ShapeDtypeStruct((blk_dev, bs, cols), jnp.float32),
        jax.ShapeDtypeStruct((n_out, bs, cols), jnp.bfloat16),
    )
    return pl.pallas_call(
        last_kernel if last else step_kernel,
        out_shape=shapes[:2] if last else shapes,
        in_specs=[smem, smem, vmem, vmem, vmem],
        out_specs=(vmem, vmem) if last else (vmem, vmem, hbm),
        scratch_shapes=[
            pltpu.VMEM((width, cols), jnp.bfloat16),
            pltpu.SemaphoreType.DMA((n_out,)),
        ],
        input_output_aliases={4: 1},
    )(take, send, arrived, coefs_wide, squares)


def send_kernel(send_ref, present_ref, out_hbm, sems):
    copies = []
    for v in range(out_hbm.shape[0]):
        cp = pltpu.make_async_copy(present_ref.at[send_ref[v]], out_hbm.at[v], sems.at[v])
        cp.start()
        copies.append(cp)
    for cp in copies:
        cp.wait()


def first_outgoing(send, present):
    n_out = send.shape[0]
    return pl.pallas_call(
        send_kernel,
        out_shape=jax.ShapeDtypeStruct((n_out,) + present.shape[1:], present.dtype),
        in_specs=[pl.BlockSpec(memory_space=pltpu.SMEM), pl.BlockSpec(memory_space=pltpu.VMEM)],
        out_specs=pl.BlockSpec(memory_space=pl.ANY),
        scratch_shapes=[pltpu.SemaphoreType.DMA((n_out,))],
    )(send, present)


def gather_rows(chosen, chosen_idio, owners):
    shocks, factors = chosen.shape
    per = shocks // owners
    packed = jnp.concatenate(
        [
            chosen.reshape(owners, per, factors),
            jnp.pad(chosen_idio.reshape(owners, 1, per), ((0, 0), (0, 0), (0, factors - per))),
        ],
        axis=1,
    )
    arrived = lax.all_to_all(packed, BOX, 0, 0, tiled=True)
    reduced = jnp.sum(arrived, axis=0, keepdims=True)
    spread = jnp.broadcast_to(reduced, packed.shape)
    full = lax.all_to_all(spread, BOX, 0, 0, tiled=True)
    return full[:, :per, :].reshape(shocks, factors), full[:, per, :per].reshape(shocks)


def make_body(zh, xs):
    zsrc_t, group_t, pos_t, perm_in, perm_out, perm_x = layout(zh, xs)

    def on_device(coefs, lag_pattern, loadings, idiosyncratic, shocked):
        loadings, idiosyncratic = lax.ppermute((loadings, idiosyncratic), ALL, perm_in)
        coefs = lax.ppermute(coefs, ALL, perm_in)
        blk_dev = coefs.shape[0]
        lags = coefs.shape[1]
        block_size = coefs.shape[2]
        k = lax.axis_index("zh")
        zl = lax.axis_index("zl")
        y = lax.axis_index("y")
        c = lax.axis_index("c")
        x = lax.axis_index("x")
        owners = ZL * YS * CORE * xs
        mine = (jnp.asarray(zsrc_t)[k, zl, y, c, x] * YS + y) * CORE + c
        group_of_pos = jnp.asarray(group_t)[k]
        pos_of_group = jnp.asarray(pos_t)[k]
        n_blocks = owners * blk_dev
        capacity = min(blk_dev, max(1, blk_dev * lags // owners))
        shifted = jnp.stack([shocked] + [lax.ppermute(shocked, ALL, perm_x[j]) for j in range(1, xs)])
        shock_columns = shocked.shape[0]
        shocked = shifted[(x - k) % xs]
        local_rows = blk_dev * block_size
        row_ids = mine * local_rows + jnp.arange(local_rows, dtype=jnp.int32)
        pick_table = (shocked[:, None] == row_ids[None, :]).astype(jnp.float32)
        chosen = jnp.dot(
            pick_table, loadings, precision=lax.Precision.HIGHEST, preferred_element_type=jnp.float32
        )
        chosen_idio = jnp.dot(
            pick_table,
            idiosyncratic,
            precision=lax.Precision.HIGHEST,
            preferred_element_type=jnp.float32,
        )
        chosen, chosen_idio = gather_rows(chosen, chosen_idio, owners)
        scale = jnp.sqrt(jnp.sum(chosen * chosen, axis=1) + chosen_idio)
        impact = jnp.dot(
            loadings, chosen.T, precision=lax.Precision.HIGHEST, preferred_element_type=jnp.float32
        )
        impact = impact + pick_table.T * idiosyncratic[:, None]
        impact = impact / scale[None, :]
        present_response = impact.astype(jnp.bfloat16).reshape(blk_dev, block_size, shock_columns)
        squared_terms = present_response.astype(jnp.float32) ** 2
        my_lags = lax.dynamic_slice_in_dim(lag_pattern, mine * blk_dev, blk_dev, 0)
        flat_lags = my_lags.reshape(-1)
        all_blocks_ids = jnp.arange(n_blocks, dtype=jnp.int32)
        read_need = jnp.any(flat_lags[:, None] == all_blocks_ids[None, :], axis=0).astype(jnp.int32)
        read_need = read_need.reshape(owners, blk_dev)[group_of_pos]
        read_before = jnp.cumsum(read_need, axis=1) - read_need
        owner_base = jnp.arange(owners, dtype=jnp.int32)[:, None] * capacity
        slot_of_pos = (owner_base + read_before).reshape(-1)
        block_at = pos_of_group[flat_lags // blk_dev] * blk_dev + flat_lags % blk_dev
        take_index = slot_of_pos[block_at]
        reader_slots = lag_pattern.reshape(owners, blk_dev * lags)[group_of_pos]
        own_ids = mine * blk_dev + jnp.arange(blk_dev, dtype=jnp.int32)
        send_need = jnp.any(reader_slots[:, :, None] == own_ids[None, None, :], axis=1).astype(
            jnp.int32
        )
        send_idx = jnp.argmax(send_need, axis=1).astype(jnp.int32)
        outgoing = first_outgoing(send_idx, present_response)
        coefs_wide = coefs.transpose(0, 2, 1, 3).reshape(blk_dev, block_size, lags * block_size)
        for step_no in range(HORIZONS - 1):
            arriving_response = lax.all_to_all(outgoing, BOX, split_axis=0, concat_axis=0, tiled=True)
            made = step(
                take_index, send_idx, arriving_response, coefs_wide, squared_terms,
                last=step_no == HORIZONS - 2,
            )
            present_response, squared_terms = made[:2]
            outgoing = made[-1]
        partial = jnp.sum(squared_terms, axis=2)
        squared_terms, partial = lax.ppermute((squared_terms, partial), ALL, perm_out)
        totals = lax.psum(partial, "x")
        total_shocks = shock_columns * xs
        shares = total_shocks * squared_terms / (totals[:, :, None] + 1e-06)
        return shares.reshape(local_rows, shock_columns)

    return on_device


def solution(mesh):
    rows = mesh.shape["rows"]
    xs = mesh.shape["shock"]
    zh = rows // (ZL * YS * CORE)
    mesh5 = Mesh(mesh.devices.reshape(zh, ZL, YS, CORE, xs), ALL)
    rows_axes = ("zh", "zl", "y", "c")
    placed = (
        P(rows_axes, None, None, None),
        P(),
        P(rows_axes, None),
        P(rows_axes),
        P("x"),
    )
    return jax.shard_map(
        make_body(zh, xs), mesh=mesh5, in_specs=placed, out_specs=P(rows_axes, "x"), check_vma=False
    )
```
